128 devices in a mesh: dp: 4 (over y_hi, core), head: 4 (over x), ctx: 8 (over z, y_lo).
Axes of the slice: x: 4, y: 4 (y_hi: 2, y_lo: 2; y = y_hi * 2 + y_lo), z: 4, core: 2. Of those that a mesh axis runs over, the one named last changes fastest.
Arguments:
- video: bfloat16 [16, 64, 24576], P('dp', 'head', 'ctx'), parts along dimension 0, may hold values from -6 to 6
- cache: bfloat16 [8, 64, 24576], P('dp', 'head', 'ctx'), parts along dimension 0, may hold values from -6 to 6
- conv_weight: bfloat16 [3, 3, 288, 192], replicated, may hold values from -0.125 to 0.125
- conv_bias: float32 [192], replicated, may hold values from -3 to 3
- down_weight: bfloat16 [768, 192], replicated, may hold values from -0.21875 to 0.21875
- patch_weight: bfloat16 [768, 5120], P(None, ('head', 'ctx')), may hold values from -0.21875 to 0.21875
- step_index: int32 [4], P('dp'), parts along dimension 0, may hold values from 0 to 999
- mod_weight: bfloat16 [256, 10240], P(None, ('head', 'ctx')), may hold values from -1 to 1
- qkv_weight: bfloat16 [5120, 20, 3, 128], P('ctx', 'head'), may hold values from -0.078125 to 0.078125
Outputs:
- attended: bfloat16 [16384, 2560], P(('dp', 'ctx'), 'head'), parts along dimension 0
The draws below stay inside these ranges and needn't reach their ends.
There are 4 independent parts, one for each index of `dp`. The reference program is written for one: setup_inputs(seed, part) draws one part's arguments, and reference() takes and returns one part's arrays. A program takes and returns all parts, laid end to end along the dimension named above; an argument that names none is the same for every part. Nothing has to cross between parts.
All inputs are finite; a program needn't handle non-finite values.
Results may differ from the reference program's by a relative error of at most 0.015.
The reference program's roundings to bfloat16 on the way (of `frames`, `hidden`, `reduced`, `patches`, `timing`, `normed`, `qkv` and `weights`) count: a program that leaves them out, or rounds other values in their place, can miss the bound.
Values may be sent and summed in bfloat16 or wider, within the bound.
No kernel may reach another device: no remote copies, remote signals or barrier semaphores. Data moves between devices by JAX's collectives and lax.ppermute only.
A program may use at most 128 MiB of HBM per device.

```python
import jax
import jax.numpy as jnp
from jax import lax

D = 5120
HDIM = 128
CIN = 96
CMID = 192
FREQ = 256
FR = 4
TR = 16
TC = 32
HEADS = 20
ROWS = 64
COLS = 256
TOKENS = 4096
N_HEAD = 4
N_CTX = 8


def draw_mod_weight(key, part):
    base = jnp.clip(jax.random.normal(key, (FREQ, 2 * D), jnp.float32), -5.0, 5.0)
    spread = 0.045
    return (base * spread).astype(jnp.bfloat16)


def steps_of(rng, dims, shards, smallest, high):
    loudness = 1.0
    for axis_at, shards_of in shards:
        steps = jax.random.uniform(jax.random.fold_in(jax.random.fold_in(rng, 6), axis_at), (shards_of,), jnp.float32, smallest / len(shards), high / len(shards))
        loudness = loudness * jnp.repeat(jnp.exp(steps), dims[axis_at] // shards_of).reshape((-1,) + (1,) * (len(dims) - 1 - axis_at))
    return loudness


def noise(own_key, extent, width, bound, cuts=(), kind=jnp.bfloat16):
    loudness = steps_of(own_key, extent, cuts, -0.22, 0.18) if cuts else 1.0
    values = jax.random.normal(own_key, extent, jnp.float32) * width * loudness
    return jnp.minimum(jnp.maximum(values, -bound), bound).astype(kind)


def setup_inputs(seed: int = 0, part: int = 0) -> dict:
    splits = jax.random.split(jax.random.key(seed), 10)
    part_splits = jax.random.split(jax.random.fold_in(splits[9], part), 10)
    return {
        "video": noise(part_splits[0], (FR, ROWS, COLS * CIN), 1.0, 6.0, ((1, 4), (2, 8))),
        "cache": noise(part_splits[1], (2, ROWS, COLS * CIN), 1.0, 6.0, ((1, 4), (2, 8))),
        "conv_weight": noise(splits[2], (3, 3, 3 * CIN, CMID), (27 * CIN) ** -0.5, 0.125),
        "conv_bias": noise(splits[3], (CMID,), 0.5, 3.0, (), jnp.float32),
        "down_weight": noise(splits[4], (4 * CMID, CMID), (4 * CMID) ** -0.5, 0.21875),
        "patch_weight": noise(splits[5], (4 * CMID, D), (4 * CMID) ** -0.5, 0.21875, ((1, 32),)),
        "step_index": jax.random.randint(part_splits[6], (1,), 0, 1000).astype(jnp.int32),
        "mod_weight": draw_mod_weight(jax.random.fold_in(splits[9], 71), part),
        "qkv_weight": noise(splits[8], (D, HEADS, 3, HDIM), D ** -0.5, 0.078125, ((0, 8), (1, 4))),
    }


def silu_act(value):
    return value * jax.nn.sigmoid(value)

def reference(video, cache, conv_weight, conv_bias, down_weight, patch_weight, step_index, mod_weight, qkv_weight):
    rows = ROWS
    cols = COLS
    frames = jnp.concatenate([cache, video], 0).reshape(FR + 2, rows, cols, CIN)
    padded = jnp.pad(frames, ((0, 0), (1, 1), (1, 1), (0, 0)))
    total = jnp.zeros((FR, rows, cols, CMID), jnp.float32)
    for time_tap in range(3):
        for row_tap in range(3):
            slab = padded[time_tap:time_tap + FR, row_tap:row_tap + rows]
            stacked = jnp.concatenate([slab[:, :, col_tap:col_tap + cols] for col_tap in range(3)], -1)
            total = total + jnp.einsum('fyxc,cd->fyxd', stacked.astype(jnp.float32), conv_weight[time_tap, row_tap].astype(jnp.float32))
    hidden = silu_act(total + conv_bias).astype(jnp.bfloat16)
    stacked = hidden.reshape(FR, rows // 2, 2, cols // 2, 2, CMID).transpose(0, 1, 3, 2, 4, 5).reshape(-1, 4 * CMID)
    reduced = silu_act(jnp.dot(stacked, down_weight, preferred_element_type=jnp.float32)).astype(jnp.bfloat16)
    reduced = reduced.reshape(FR, rows // 2, cols // 2, CMID)
    patches = reduced.reshape(FR, rows // 4, 2, cols // 4, 2, CMID).transpose(0, 1, 3, 2, 4, 5)
    patches = patches.reshape(FR, N_HEAD, TR // 4, N_CTX, TC // 4, 4 * CMID).transpose(3, 1, 0, 2, 4, 5)
    patches = patches.reshape(TOKENS, 4 * CMID)
    embedded = jnp.dot(patches, patch_weight, preferred_element_type=jnp.float32)
    half = FREQ // 2
    freqs = jnp.exp(-jnp.log(10000.0) * jnp.arange(half, dtype=jnp.float32) / half)
    angles = step_index[0].astype(jnp.float32) * freqs
    timing = jnp.concatenate([jnp.cos(angles), jnp.sin(angles)]).astype(jnp.bfloat16)
    modulation = jnp.dot(timing[None, :], mod_weight, preferred_element_type=jnp.float32)[0]
    scale = modulation[:D]
    shift = modulation[D:]
    inverse = lax.rsqrt(lax.optimization_barrier(jnp.mean(embedded * embedded, -1, keepdims=True)) + 1e-06)
    normed = (embedded * inverse * (1.0 + scale) + shift).astype(jnp.bfloat16)
    qkv = jnp.dot(normed, qkv_weight.reshape(D, -1), preferred_element_type=jnp.float32).astype(jnp.bfloat16)
    qkv = qkv.reshape(TOKENS, HEADS, 3, HDIM).transpose(1, 2, 0, 3)

    def one_head(triple):
        query, keys, values = (triple[0], triple[1], triple[2])
        scores = jnp.dot(query, keys.T, preferred_element_type=jnp.float32) / jnp.sqrt(jnp.float32(HDIM))
        top = lax.optimization_barrier(jnp.max(scores, -1, keepdims=True))
        probs = jnp.exp(scores - top)
        denom = lax.optimization_barrier(jnp.sum(probs, -1, keepdims=True))
        weights = probs.astype(jnp.bfloat16)
        return (jnp.dot(weights, values, preferred_element_type=jnp.float32) / denom).astype(jnp.bfloat16)
    heads_out = lax.map(one_head, qkv)
    return heads_out.transpose(1, 0, 2).reshape(TOKENS, HEADS * HDIM)
```

```python
import jax
import jax.numpy as jnp
from jax import lax
from jax.sharding import PartitionSpec as P

D = 5120
HDIM = 128
FREQ = 256


def with_halo(cells, sides, width):
    for axis, dim in sides:
        count = lax.axis_size(axis)
        ends = count - 1
        head = lax.slice_in_dim(cells, 0, width, axis=dim)
        tail = lax.slice_in_dim(cells, cells.shape[dim] - width, cells.shape[dim], axis=dim)
        cells = jnp.concatenate(
            [
                lax.ppermute(tail, axis, [(i, (i + 1) % count) for i in range(ends)]),
                cells,
                lax.ppermute(head, axis, [((i + 1) % count, i) for i in range(ends)]),
            ],
            axis=dim,
        )
    return cells


def silu_act(value):
    return value * jax.nn.sigmoid(value)


def shards(
    video,
    cache,
    conv_weight,
    conv_bias,
    down_weight,
    patch_weight,
    step_index,
    mod_weight,
    qkv_weight,
):
    cin = conv_weight.shape[2] // 3
    cmid = conv_weight.shape[3]
    frame_count = video.shape[0]
    tile_rows = video.shape[1]
    tile_cols = video.shape[2] // cin
    frames = jnp.concatenate([cache, video], 0).reshape(frame_count + 2, tile_rows, tile_cols, cin)
    padded = with_halo(frames, (("head", 1), ("ctx", 2)), 1)
    total = jnp.zeros((frame_count, tile_rows, tile_cols, cmid), jnp.float32)
    for time_tap in range(3):
        for row_tap in range(3):
            slab = padded[time_tap : time_tap + frame_count, row_tap : row_tap + tile_rows]
            stacked = jnp.concatenate(
                [slab[:, :, col_tap : col_tap + tile_cols] for col_tap in range(3)], -1
            )
            total = total + jnp.einsum(
                "fyxc,cd->fyxd",
                stacked,
                conv_weight[time_tap, row_tap],
                preferred_element_type=jnp.float32,
            )
    hidden = silu_act(total + conv_bias).astype(jnp.bfloat16)
    stacked = (
        hidden.reshape(frame_count, tile_rows // 2, 2, tile_cols // 2, 2, cmid)
        .transpose(0, 1, 3, 2, 4, 5)
        .reshape(-1, 4 * cmid)
    )
    reduced = silu_act(jnp.dot(stacked, down_weight, preferred_element_type=jnp.float32)).astype(
        jnp.bfloat16
    )
    reduced = reduced.reshape(frame_count, tile_rows // 2, tile_cols // 2, cmid)
    patches = reduced.reshape(frame_count, tile_rows // 4, 2, tile_cols // 4, 2, cmid).transpose(
        0, 1, 3, 2, 4, 5
    )
    patches = patches.reshape(-1, 4 * cmid)
    half = FREQ // 2
    freqs = jnp.exp(-jnp.log(10000.0) * jnp.arange(half, dtype=jnp.float32) / half)
    angles = step_index[0].astype(jnp.float32) * freqs
    timing = jnp.concatenate([jnp.cos(angles), jnp.sin(angles)]).astype(jnp.bfloat16)
    mod_share = jnp.dot(timing[None, :], mod_weight, preferred_element_type=jnp.float32)[0]
    modulation = lax.all_gather(
        lax.all_gather(mod_share, "ctx", axis=0, tiled=True), "head", axis=0, tiled=True
    )
    n_head = lax.axis_size("head")
    n_ctx = lax.axis_size("ctx")
    h_idx = lax.axis_index("head")
    c_idx = lax.axis_index("ctx")
    quarter = D // n_head
    scale = lax.dynamic_slice_in_dim(modulation, h_idx * quarter, quarter)
    shift = lax.dynamic_slice_in_dim(modulation, D + h_idx * quarter, quarter)
    weight_quarter = lax.all_gather(patch_weight, "ctx", axis=1, tiled=True)
    block_patches = lax.all_gather(patches, "head", axis=0, tiled=True)
    embedded = jnp.dot(block_patches, weight_quarter, preferred_element_type=jnp.float32)
    squares = lax.all_gather(jnp.sum(embedded * embedded, -1), "head", axis=0, tiled=False)
    inverse = lax.rsqrt(jnp.sum(squares, 0) / D + 1e-06)[:, None]
    normed_quarter = (embedded * inverse * (1.0 + scale) + shift).astype(jnp.bfloat16)
    normed = lax.all_gather(normed_quarter, "head", axis=1, tiled=True)
    group_rows = normed.shape[0]
    heads_here = qkv_weight.shape[1]
    out_cols = heads_here * 3 * HDIM
    local = qkv_weight.reshape(qkv_weight.shape[0], out_cols)
    rows = local.shape[0]
    half_rows = rows // 2
    core = lax.axis_index("dp") % 2
    mine = lax.dynamic_slice_in_dim(local, core * half_rows, half_rows, 0)
    fetched = jnp.stack(
        [
            lax.ppermute(mine, "ctx", [(i, (i + s) % n_ctx) for i in range(n_ctx)])
            for s in range(1, n_ctx)
        ]
    )
    n_dp = lax.axis_size("dp")
    partner = lax.ppermute(fetched, "dp", [(i, i ^ 1) for i in range(n_dp)])
    weight = jnp.concatenate(
        [local, fetched.reshape(-1, out_cols), partner.reshape(-1, out_cols)], 0
    )
    pieces = [lax.dynamic_slice_in_dim(normed, c_idx * rows, rows, 1)]
    for side in (core, 1 - core):
        for s in range(1, n_ctx):
            block = (c_idx + n_ctx - s) % n_ctx
            pieces.append(
                lax.dynamic_slice_in_dim(normed, block * rows + side * half_rows, half_rows, 1)
            )
    qkv = jnp.dot(jnp.concatenate(pieces, 1), weight, preferred_element_type=jnp.float32)
    qkv = qkv.astype(jnp.bfloat16).reshape(group_rows, heads_here, 3, HDIM)
    query = qkv[:, :, 0]
    keys = qkv[:, :, 1]
    values = qkv[:, :, 2]
    inv_root = 1.0 / jnp.sqrt(jnp.float32(HDIM))
    best = jnp.full((heads_here, group_rows), -1e30, jnp.float32)
    key_piece = lax.all_gather(keys, "ctx", axis=0, tiled=True)
    value_piece = lax.all_gather(values, "ctx", axis=0, tiled=True)
    scores = (
        jnp.einsum("qhd,khd->hqk", query, key_piece, preferred_element_type=jnp.float32) * inv_root
    )
    new_best = jnp.maximum(best, jnp.max(scores, -1))
    probs = jnp.exp(scores - new_best[..., None])
    denom = jnp.sum(probs, -1)
    accum = jnp.einsum(
        "hqk,khd->hqd", probs.astype(jnp.bfloat16), value_piece, preferred_element_type=jnp.float32
    )
    best, denom, accum = (new_best, denom, accum)
    result = (accum / denom[..., None]).astype(jnp.bfloat16)
    return result.transpose(1, 0, 2).reshape(group_rows, heads_here * HDIM)


def solution(mesh):
    return jax.shard_map(
        shards,
        mesh=mesh,
        in_specs=(
            P("dp", "head", "ctx"),
            P("dp", "head", "ctx"),
            P(),
            P(),
            P(),
            P(None, ("head", "ctx")),
            P("dp"),
            P(None, ("head", "ctx")),
            P("ctx", "head", None, None),
        ),
        out_specs=P(("dp", "ctx"), "head"),
        check_vma=False,
    )
```

```python
import jax
import jax.numpy as jnp
from jax import lax
from jax.sharding import PartitionSpec as P

D = 5120
HDIM = 128
FREQ = 256


def with_halo(cells, sides, width):
    for axis, dim in sides:
        count = lax.axis_size(axis)
        ends = count - 1
        head = lax.slice_in_dim(cells, 0, width, axis=dim)
        tail = lax.slice_in_dim(cells, cells.shape[dim] - width, cells.shape[dim], axis=dim)
        cells = jnp.concatenate(
            [
                lax.ppermute(tail, axis, [(i, (i + 1) % count) for i in range(ends)]),
                cells,
                lax.ppermute(head, axis, [((i + 1) % count, i) for i in range(ends)]),
            ],
            axis=dim,
        )
    return cells


def gather_rows(cells, axis):
    count = lax.axis_size(axis)
    me = lax.axis_index(axis)
    parts = [cells] + [
        lax.ppermute(cells, axis, [(i, (i + s) % count) for i in range(count)])
        for s in range(1, count)
    ]
    stacked = jnp.stack(parts)
    return jnp.take(stacked, (me - jnp.arange(count)) % count, axis=0)


def silu_act(value):
    return value * jax.nn.sigmoid(value)


def shards(
    video,
    cache,
    conv_weight,
    conv_bias,
    down_weight,
    patch_weight,
    step_index,
    mod_weight,
    qkv_weight,
):
    cin = conv_weight.shape[2] // 3
    cmid = conv_weight.shape[3]
    frame_count = video.shape[0]
    tile_rows = video.shape[1]
    tile_cols = video.shape[2] // cin
    frames = jnp.concatenate([cache, video], 0).reshape(frame_count + 2, tile_rows, tile_cols, cin)
    padded = with_halo(frames, (("head", 1), ("ctx", 2)), 1)
    total = jnp.zeros((frame_count, tile_rows, tile_cols, cmid), jnp.float32)
    for time_tap in range(3):
        for row_tap in range(3):
            slab = padded[time_tap : time_tap + frame_count, row_tap : row_tap + tile_rows]
            stacked = jnp.concatenate(
                [slab[:, :, col_tap : col_tap + tile_cols] for col_tap in range(3)], -1
            )
            total = total + jnp.einsum(
                "fyxc,cd->fyxd",
                stacked,
                conv_weight[time_tap, row_tap],
                preferred_element_type=jnp.float32,
            )
    hidden = silu_act(total + conv_bias).astype(jnp.bfloat16)
    stacked = (
        hidden.reshape(frame_count, tile_rows // 2, 2, tile_cols // 2, 2, cmid)
        .transpose(0, 1, 3, 2, 4, 5)
        .reshape(-1, 4 * cmid)
    )
    reduced = silu_act(jnp.dot(stacked, down_weight, preferred_element_type=jnp.float32)).astype(
        jnp.bfloat16
    )
    reduced = reduced.reshape(frame_count, tile_rows // 2, tile_cols // 2, cmid)
    patches = reduced.reshape(frame_count, tile_rows // 4, 2, tile_cols // 4, 2, cmid).transpose(
        0, 1, 3, 2, 4, 5
    )
    patches = patches.reshape(-1, 4 * cmid)
    half = FREQ // 2
    freqs = jnp.exp(-jnp.log(10000.0) * jnp.arange(half, dtype=jnp.float32) / half)
    angles = step_index[0].astype(jnp.float32) * freqs
    timing = jnp.concatenate([jnp.cos(angles), jnp.sin(angles)]).astype(jnp.bfloat16)
    mod_share = jnp.dot(timing[None, :], mod_weight, preferred_element_type=jnp.float32)[0]
    modulation = gather_rows(gather_rows(mod_share, "ctx").reshape(-1), "head").reshape(-1)
    n_head = lax.axis_size("head")
    n_ctx = lax.axis_size("ctx")
    h_idx = lax.axis_index("head")
    c_idx = lax.axis_index("ctx")
    quarter = D // n_head
    scale = lax.dynamic_slice_in_dim(modulation, h_idx * quarter, quarter)
    shift = lax.dynamic_slice_in_dim(modulation, D + h_idx * quarter, quarter)
    weight_quarter = lax.all_gather(patch_weight, "ctx", axis=1, tiled=True)
    block_patches = gather_rows(patches, "head").reshape(-1, patches.shape[1])
    embedded = jnp.dot(block_patches, weight_quarter, preferred_element_type=jnp.float32)
    squares = gather_rows(jnp.sum(embedded * embedded, -1), "head")
    inverse = lax.rsqrt(jnp.sum(squares, 0) / D + 1e-06)[:, None]
    normed_quarter = (embedded * inverse * (1.0 + scale) + shift).astype(jnp.bfloat16)
    normed = lax.all_gather(normed_quarter, "head", axis=1, tiled=True)
    group_rows = normed.shape[0]
    heads_here = qkv_weight.shape[1]
    out_cols = heads_here * 3 * HDIM
    local = qkv_weight.reshape(qkv_weight.shape[0], out_cols)
    rows = local.shape[0]
    half_rows = rows // 2
    core = lax.axis_index("dp") % 2
    mine = lax.dynamic_slice_in_dim(local, core * half_rows, half_rows, 0)
    fetched = jnp.stack(
        [
            lax.ppermute(mine, "ctx", [(i, (i + s) % n_ctx) for i in range(n_ctx)])
            for s in range(1, n_ctx)
        ]
    )
    n_dp = lax.axis_size("dp")
    partner = lax.ppermute(fetched, "dp", [(i, i ^ 1) for i in range(n_dp)])
    weight = jnp.concatenate(
        [local, fetched.reshape(-1, out_cols), partner.reshape(-1, out_cols)], 0
    )
    pieces = [lax.dynamic_slice_in_dim(normed, c_idx * rows, rows, 1)]
    for side in (core, 1 - core):
        for s in range(1, n_ctx):
            block = (c_idx + n_ctx - s) % n_ctx
            pieces.append(
                lax.dynamic_slice_in_dim(normed, block * rows + side * half_rows, half_rows, 1)
            )
    qkv = jnp.dot(jnp.concatenate(pieces, 1), weight, preferred_element_type=jnp.float32)
    qkv = qkv.astype(jnp.bfloat16).reshape(group_rows, heads_here, 3, HDIM)
    query = qkv[:, :, 0]
    keys = qkv[:, :, 1]
    values = qkv[:, :, 2]
    inv_root = 1.0 / jnp.sqrt(jnp.float32(HDIM))
    best = jnp.full((heads_here, group_rows), -1e30, jnp.float32)
    key_piece = lax.all_gather(keys, "ctx", axis=0, tiled=True)
    value_piece = lax.all_gather(values, "ctx", axis=0, tiled=True)
    scores = (
        jnp.einsum("qhd,khd->hqk", query, key_piece, preferred_element_type=jnp.float32) * inv_root
    )
    new_best = jnp.maximum(best, jnp.max(scores, -1))
    probs = jnp.exp(scores - new_best[..., None])
    denom = jnp.sum(probs, -1)
    accum = jnp.einsum(
        "hqk,khd->hqd", probs.astype(jnp.bfloat16), value_piece, preferred_element_type=jnp.float32
    )
    best, denom, accum = (new_best, denom, accum)
    result = (accum / denom[..., None]).astype(jnp.bfloat16)
    return result.transpose(1, 0, 2).reshape(group_rows, heads_here * HDIM)


def solution(mesh):
    return jax.shard_map(
        shards,
        mesh=mesh,
        in_specs=(
            P("dp", "head", "ctx"),
            P("dp", "head", "ctx"),
            P(),
            P(),
            P(),
            P(None, ("head", "ctx")),
            P("dp"),
            P(None, ("head", "ctx")),
            P("ctx", "head", None, None),
        ),
        out_specs=P(("dp", "ctx"), "head"),
        check_vma=False,
    )
```

```python
import jax
import jax.numpy as jnp
from jax import lax
from jax.sharding import PartitionSpec as P

D = 5120
HDIM = 128
FREQ = 256


def with_halo(cells, sides, width):
    for axis, dim in sides:
        count = lax.axis_size(axis)
        ends = count - 1
        head = lax.slice_in_dim(cells, 0, width, axis=dim)
        tail = lax.slice_in_dim(cells, cells.shape[dim] - width, cells.shape[dim], axis=dim)
        cells = jnp.concatenate(
            [
                lax.ppermute(tail, axis, [(i, (i + 1) % count) for i in range(ends)]),
                cells,
                lax.ppermute(head, axis, [((i + 1) % count, i) for i in range(ends)]),
            ],
            axis=dim,
        )
    return cells


def gather_rows(cells, axis):
    count = lax.axis_size(axis)
    me = lax.axis_index(axis)
    parts = [cells] + [
        lax.ppermute(cells, axis, [(i, (i + s) % count) for i in range(count)])
        for s in range(1, count)
    ]
    stacked = jnp.stack(parts)
    return jnp.take(stacked, (me - jnp.arange(count)) % count, axis=0)


def silu_act(value):
    return value * jax.nn.sigmoid(value)


def shards(
    video,
    cache,
    conv_weight,
    conv_bias,
    down_weight,
    patch_weight,
    step_index,
    mod_weight,
    qkv_weight,
):
    cin = conv_weight.shape[2] // 3
    cmid = conv_weight.shape[3]
    frame_count = video.shape[0]
    tile_rows = video.shape[1]
    tile_cols = video.shape[2] // cin
    frames = jnp.concatenate([cache, video], 0).reshape(frame_count + 2, tile_rows, tile_cols, cin)
    padded = with_halo(frames, (("head", 1), ("ctx", 2)), 1)
    total = jnp.zeros((frame_count, tile_rows, tile_cols, cmid), jnp.float32)
    for time_tap in range(3):
        for row_tap in range(3):
            slab = padded[time_tap : time_tap + frame_count, row_tap : row_tap + tile_rows]
            stacked = jnp.concatenate(
                [slab[:, :, col_tap : col_tap + tile_cols] for col_tap in range(3)], -1
            )
            total = total + jnp.einsum(
                "fyxc,cd->fyxd",
                stacked,
                conv_weight[time_tap, row_tap],
                preferred_element_type=jnp.float32,
            )
    hidden = silu_act(total + conv_bias).astype(jnp.bfloat16)
    stacked = (
        hidden.reshape(frame_count, tile_rows // 2, 2, tile_cols // 2, 2, cmid)
        .transpose(0, 1, 3, 2, 4, 5)
        .reshape(-1, 4 * cmid)
    )
    reduced = silu_act(jnp.dot(stacked, down_weight, preferred_element_type=jnp.float32)).astype(
        jnp.bfloat16
    )
    reduced = reduced.reshape(frame_count, tile_rows // 2, tile_cols // 2, cmid)
    patches = reduced.reshape(frame_count, tile_rows // 4, 2, tile_cols // 4, 2, cmid).transpose(
        0, 1, 3, 2, 4, 5
    )
    patches = patches.reshape(-1, 4 * cmid)
    half = FREQ // 2
    freqs = jnp.exp(-jnp.log(10000.0) * jnp.arange(half, dtype=jnp.float32) / half)
    angles = step_index[0].astype(jnp.float32) * freqs
    timing = jnp.concatenate([jnp.cos(angles), jnp.sin(angles)]).astype(jnp.bfloat16)
    mod_share = jnp.dot(timing[None, :], mod_weight, preferred_element_type=jnp.float32)[0]
    modulation = gather_rows(gather_rows(mod_share, "ctx").reshape(-1), "head").reshape(-1)
    n_head = lax.axis_size("head")
    n_ctx = lax.axis_size("ctx")
    h_idx = lax.axis_index("head")
    c_idx = lax.axis_index("ctx")
    quarter = D // n_head
    scale = lax.dynamic_slice_in_dim(modulation, h_idx * quarter, quarter)
    shift = lax.dynamic_slice_in_dim(modulation, D + h_idx * quarter, quarter)
    weight_quarter = lax.all_gather(patch_weight, "ctx", axis=1, tiled=True)
    block_patches = gather_rows(patches, "head").reshape(-1, patches.shape[1])
    embedded = jnp.dot(block_patches, weight_quarter, preferred_element_type=jnp.float32)
    squares = gather_rows(jnp.sum(embedded * embedded, -1), "head")
    inverse = lax.rsqrt(jnp.sum(squares, 0) / D + 1e-06)[:, None]
    normed_quarter = (embedded * inverse * (1.0 + scale) + shift).astype(jnp.bfloat16)
    normed = lax.all_gather(normed_quarter, "head", axis=1, tiled=True)
    group_rows = normed.shape[0]
    heads_here = qkv_weight.shape[1]
    out_cols = heads_here * 3 * HDIM
    local = qkv_weight.reshape(qkv_weight.shape[0], out_cols)
    rows = local.shape[0]
    half_rows = rows // 2
    core = lax.axis_index("dp") % 2
    mine = lax.dynamic_slice_in_dim(local, core * half_rows, half_rows, 0)
    fetched = jnp.stack(
        [
            lax.ppermute(mine, "ctx", [(i, (i + s) % n_ctx) for i in range(n_ctx)])
            for s in range(1, n_ctx)
        ]
    )
    n_dp = lax.axis_size("dp")
    partner = lax.ppermute(fetched, "dp", [(i, i ^ 1) for i in range(n_dp)])
    weight = jnp.concatenate(
        [local, fetched.reshape(-1, out_cols), partner.reshape(-1, out_cols)], 0
    )
    pieces = [lax.dynamic_slice_in_dim(normed, c_idx * rows, rows, 1)]
    for side in (core, 1 - core):
        for s in range(1, n_ctx):
            block = (c_idx + n_ctx - s) % n_ctx
            pieces.append(
                lax.dynamic_slice_in_dim(normed, block * rows + side * half_rows, half_rows, 1)
            )
    qkv = jnp.dot(jnp.concatenate(pieces, 1), weight, preferred_element_type=jnp.float32)
    qkv = qkv.astype(jnp.bfloat16).reshape(group_rows, heads_here, 3, HDIM)
    active = min(heads_here, n_ctx)
    received = [lax.dynamic_index_in_dim(qkv, jnp.minimum(c_idx, active - 1), 1, keepdims=False)]
    for s in range(1, n_ctx):
        target = jnp.minimum((c_idx + s) % n_ctx, active - 1)
        received.append(
            lax.ppermute(
                lax.dynamic_index_in_dim(qkv, target, 1, keepdims=False),
                "ctx",
                [(b, (b + s) % n_ctx) for b in range(n_ctx) if (b + s) % n_ctx < active],
            )
        )
    triple = jnp.stack(received)
    keys = triple[:, :, 1].reshape(-1, HDIM)
    values = triple[:, :, 2].reshape(-1, HDIM)
    inv_root = 1.0 / jnp.sqrt(jnp.float32(HDIM))

    def one_block(query):
        scores = jnp.dot(query, keys.T, preferred_element_type=jnp.float32) * inv_root
        best = jnp.maximum(jnp.float32(-1e30), jnp.max(scores, -1))
        probs = jnp.exp(scores - best[:, None])
        denom = jnp.sum(probs, -1)
        accum = jnp.dot(probs.astype(jnp.bfloat16), values, preferred_element_type=jnp.float32)
        return (accum / denom[:, None]).astype(jnp.bfloat16)

    attended = lax.map(one_block, triple[:, :, 0])
    returned = [attended[0]]
    for s in range(1, n_ctx):
        returned.append(
            lax.ppermute(attended[s], "ctx", [(d, (d - s) % n_ctx) for d in range(active)])
        )
    by_head = jnp.take(jnp.stack(returned), (jnp.arange(heads_here) - c_idx) % n_ctx, axis=0)
    return by_head.transpose(1, 0, 2).reshape(group_rows, heads_here * HDIM)


def solution(mesh):
    return jax.shard_map(
        shards,
        mesh=mesh,
        in_specs=(
            P("dp", "head", "ctx"),
            P("dp", "head", "ctx"),
            P(),
            P(),
            P(),
            P(None, ("head", "ctx")),
            P("dp"),
            P(None, ("head", "ctx")),
            P("ctx", "head", None, None),
        ),
        out_specs=P(("dp", "ctx"), "head"),
        check_vma=False,
    )
```

```python
import jax
import jax.numpy as jnp
from jax import lax
from jax.sharding import PartitionSpec as P

D = 5120
HDIM = 128
FREQ = 256


def with_halo(cells, sides, width):
    for axis, dim in sides:
        count = lax.axis_size(axis)
        ends = count - 1
        head = lax.slice_in_dim(cells, 0, width, axis=dim)
        tail = lax.slice_in_dim(cells, cells.shape[dim] - width, cells.shape[dim], axis=dim)
        cells = jnp.concatenate(
            [
                lax.ppermute(tail, axis, [(i, (i + 1) % count) for i in range(ends)]),
                cells,
                lax.ppermute(head, axis, [((i + 1) % count, i) for i in range(ends)]),
            ],
            axis=dim,
        )
    return cells


def gather_rows(cells, axis):
    count = lax.axis_size(axis)
    me = lax.axis_index(axis)
    parts = [cells] + [
        lax.ppermute(cells, axis, [(i, (i + s) % count) for i in range(count)])
        for s in range(1, count)
    ]
    stacked = jnp.stack(parts)
    return jnp.take(stacked, (me - jnp.arange(count)) % count, axis=0)


def silu_act(value):
    return value * jax.nn.sigmoid(value)


def shards(
    video,
    cache,
    conv_weight,
    conv_bias,
    down_weight,
    patch_weight,
    step_index,
    mod_weight,
    qkv_weight,
):
    cin = conv_weight.shape[2] // 3
    cmid = conv_weight.shape[3]
    frame_count = video.shape[0]
    tile_rows = video.shape[1]
    tile_cols = video.shape[2] // cin
    frames = jnp.concatenate([cache, video], 0).reshape(frame_count + 2, tile_rows, tile_cols, cin)
    padded = with_halo(frames, (("head", 1), ("ctx", 2)), 1)
    total = jnp.zeros((frame_count, tile_rows, tile_cols, cmid), jnp.float32)
    for time_tap in range(3):
        for row_tap in range(3):
            slab = padded[time_tap : time_tap + frame_count, row_tap : row_tap + tile_rows]
            stacked = jnp.concatenate(
                [slab[:, :, col_tap : col_tap + tile_cols] for col_tap in range(3)], -1
            )
            total = total + jnp.einsum(
                "fyxc,cd->fyxd",
                stacked,
                conv_weight[time_tap, row_tap],
                preferred_element_type=jnp.float32,
            )
    hidden = silu_act(total + conv_bias).astype(jnp.bfloat16)
    stacked = (
        hidden.reshape(frame_count, tile_rows // 2, 2, tile_cols // 2, 2, cmid)
        .transpose(0, 1, 3, 2, 4, 5)
        .reshape(-1, 4 * cmid)
    )
    reduced = silu_act(jnp.dot(stacked, down_weight, preferred_element_type=jnp.float32)).astype(
        jnp.bfloat16
    )
    reduced = reduced.reshape(frame_count, tile_rows // 2, tile_cols // 2, cmid)
    patches = reduced.reshape(frame_count, tile_rows // 4, 2, tile_cols // 4, 2, cmid).transpose(
        0, 1, 3, 2, 4, 5
    )
    patches = patches.reshape(-1, 4 * cmid)
    half = FREQ // 2
    freqs = jnp.exp(-jnp.log(10000.0) * jnp.arange(half, dtype=jnp.float32) / half)
    angles = step_index[0].astype(jnp.float32) * freqs
    timing = jnp.concatenate([jnp.cos(angles), jnp.sin(angles)]).astype(jnp.bfloat16)
    mod_share = jnp.dot(timing[None, :], mod_weight, preferred_element_type=jnp.float32)[0]
    modulation = gather_rows(gather_rows(mod_share, "ctx").reshape(-1), "head").reshape(-1)
    n_head = lax.axis_size("head")
    n_ctx = lax.axis_size("ctx")
    h_idx = lax.axis_index("head")
    c_idx = lax.axis_index("ctx")
    quarter = D // n_head
    scale = lax.dynamic_slice_in_dim(modulation, h_idx * quarter, quarter)
    shift = lax.dynamic_slice_in_dim(modulation, D + h_idx * quarter, quarter)
    weight_quarter = lax.all_gather(patch_weight, "ctx", axis=1, tiled=True)
    block_patches = gather_rows(patches, "head").reshape(-1, patches.shape[1])
    embedded = jnp.dot(block_patches, weight_quarter, preferred_element_type=jnp.float32)
    squares = gather_rows(jnp.sum(embedded * embedded, -1), "head")
    inverse = lax.rsqrt(jnp.sum(squares, 0) / D + 1e-06)[:, None]
    normed_quarter = (embedded * inverse * (1.0 + scale) + shift).astype(jnp.bfloat16)
    normed = lax.all_gather(normed_quarter, "head", axis=1, tiled=True)
    group_rows = normed.shape[0]
    heads_here = qkv_weight.shape[1]
    out_cols = heads_here * 3 * HDIM
    local = qkv_weight.reshape(qkv_weight.shape[0], out_cols)
    rows = local.shape[0]
    half_rows = rows // 2
    core = lax.axis_index("dp") % 2
    mine = lax.dynamic_slice_in_dim(local, core * half_rows, half_rows, 0)
    fetched = [
        lax.ppermute(mine, "ctx", [(i, (i + s) % n_ctx) for i in range(n_ctx)])
        for s in range(1, n_ctx)
    ]
    n_dp = lax.axis_size("dp")
    partner = [lax.ppermute(f, "dp", [(i, i ^ 1) for i in range(n_dp)]) for f in fetched]
    weight = jnp.concatenate([local] + fetched + partner, 0)
    pieces = [lax.dynamic_slice_in_dim(normed, c_idx * rows, rows, 1)]
    for side in (core, 1 - core):
        for s in range(1, n_ctx):
            block = (c_idx + n_ctx - s) % n_ctx
            pieces.append(
                lax.dynamic_slice_in_dim(normed, block * rows + side * half_rows, half_rows, 1)
            )
    qkv = jnp.dot(jnp.concatenate(pieces, 1), weight, preferred_element_type=jnp.float32)
    qkv = qkv.astype(jnp.bfloat16).reshape(group_rows, heads_here, 3, HDIM)
    active = min(heads_here, n_ctx)
    received = [lax.dynamic_index_in_dim(qkv, jnp.minimum(c_idx, active - 1), 1, keepdims=False)]
    for s in range(1, n_ctx):
        target = jnp.minimum((c_idx + s) % n_ctx, active - 1)
        received.append(
            lax.ppermute(
                lax.dynamic_index_in_dim(qkv, target, 1, keepdims=False),
                "ctx",
                [(b, (b + s) % n_ctx) for b in range(n_ctx) if (b + s) % n_ctx < active],
            )
        )
    triple = jnp.stack(received)
    keys = triple[:, :, 1].reshape(-1, HDIM)
    values = triple[:, :, 2].reshape(-1, HDIM)
    inv_root = 1.0 / jnp.sqrt(jnp.float32(HDIM))

    def one_block(query):
        scores = jnp.dot(query, keys.T, preferred_element_type=jnp.float32) * inv_root
        best = jnp.maximum(jnp.float32(-1e30), jnp.max(scores, -1))
        probs = jnp.exp(scores - best[:, None])
        denom = jnp.sum(probs, -1)
        accum = jnp.dot(probs.astype(jnp.bfloat16), values, preferred_element_type=jnp.float32)
        return (accum / denom[:, None]).astype(jnp.bfloat16)

    attended = lax.map(one_block, triple[:, :, 0])
    returned = [attended[0]]
    for s in range(1, n_ctx):
        returned.append(
            lax.ppermute(attended[s], "ctx", [(d, (d - s) % n_ctx) for d in range(active)])
        )
    by_head = jnp.take(jnp.stack(returned), (jnp.arange(heads_here) - c_idx) % n_ctx, axis=0)
    return by_head.transpose(1, 0, 2).reshape(group_rows, heads_here * HDIM)


def solution(mesh):
    return jax.shard_map(
        shards,
        mesh=mesh,
        in_specs=(
            P("dp", "head", "ctx"),
            P("dp", "head", "ctx"),
            P(),
            P(),
            P(),
            P(None, ("head", "ctx")),
            P("dp"),
            P(None, ("head", "ctx")),
            P("ctx", "head", None, None),
        ),
        out_specs=P(("dp", "ctx"), "head"),
        check_vma=False,
    )
```

```python
import jax
import jax.numpy as jnp
from jax import lax
from jax.sharding import PartitionSpec as P

D = 5120
HDIM = 128
FREQ = 256


def with_halo(cells, sides, width):
    for axis, dim in sides:
        count = lax.axis_size(axis)
        ends = count - 1
        head = lax.slice_in_dim(cells, 0, width, axis=dim)
        tail = lax.slice_in_dim(cells, cells.shape[dim] - width, cells.shape[dim], axis=dim)
        cells = jnp.concatenate(
            [
                lax.ppermute(tail, axis, [(i, (i + 1) % count) for i in range(ends)]),
                cells,
                lax.ppermute(head, axis, [((i + 1) % count, i) for i in range(ends)]),
            ],
            axis=dim,
        )
    return cells


def gather_rows(cells, axis):
    count = lax.axis_size(axis)
    me = lax.axis_index(axis)
    parts = [cells] + [
        lax.ppermute(cells, axis, [(i, (i + s) % count) for i in range(count)])
        for s in range(1, count)
    ]
    stacked = jnp.stack(parts)
    return jnp.take(stacked, (me - jnp.arange(count)) % count, axis=0)


def silu_act(value):
    return value * jax.nn.sigmoid(value)


def shards(
    video,
    cache,
    conv_weight,
    conv_bias,
    down_weight,
    patch_weight,
    step_index,
    mod_weight,
    qkv_weight,
):
    cin = conv_weight.shape[2] // 3
    cmid = conv_weight.shape[3]
    frame_count = video.shape[0]
    tile_rows = video.shape[1]
    tile_cols = video.shape[2] // cin
    frames = jnp.concatenate([cache, video], 0).reshape(frame_count + 2, tile_rows, tile_cols, cin)
    padded = with_halo(frames, (("head", 1), ("ctx", 2)), 1)
    total = jnp.zeros((frame_count, tile_rows, tile_cols, cmid), jnp.float32)
    for time_tap in range(3):
        for row_tap in range(3):
            slab = padded[time_tap : time_tap + frame_count, row_tap : row_tap + tile_rows]
            stacked = jnp.concatenate(
                [slab[:, :, col_tap : col_tap + tile_cols] for col_tap in range(3)], -1
            )
            total = total + jnp.einsum(
                "fyxc,cd->fyxd",
                stacked,
                conv_weight[time_tap, row_tap],
                preferred_element_type=jnp.float32,
            )
    hidden = silu_act(total + conv_bias).astype(jnp.bfloat16)
    stacked = (
        hidden.reshape(frame_count, tile_rows // 2, 2, tile_cols // 2, 2, cmid)
        .transpose(0, 1, 3, 2, 4, 5)
        .reshape(-1, 4 * cmid)
    )
    reduced = silu_act(jnp.dot(stacked, down_weight, preferred_element_type=jnp.float32)).astype(
        jnp.bfloat16
    )
    reduced = reduced.reshape(frame_count, tile_rows // 2, tile_cols // 2, cmid)
    patches = reduced.reshape(frame_count, tile_rows // 4, 2, tile_cols // 4, 2, cmid).transpose(
        0, 1, 3, 2, 4, 5
    )
    patches = patches.reshape(-1, 4 * cmid)
    half = FREQ // 2
    freqs = jnp.exp(-jnp.log(10000.0) * jnp.arange(half, dtype=jnp.float32) / half)
    angles = step_index[0].astype(jnp.float32) * freqs
    timing = jnp.concatenate([jnp.cos(angles), jnp.sin(angles)]).astype(jnp.bfloat16)
    mod_share = jnp.dot(timing[None, :], mod_weight, preferred_element_type=jnp.float32)[0]
    modulation = gather_rows(gather_rows(mod_share, "ctx").reshape(-1), "head").reshape(-1)
    n_head = lax.axis_size("head")
    n_ctx = lax.axis_size("ctx")
    h_idx = lax.axis_index("head")
    c_idx = lax.axis_index("ctx")
    quarter = D // n_head
    scale = lax.dynamic_slice_in_dim(modulation, h_idx * quarter, quarter)
    shift = lax.dynamic_slice_in_dim(modulation, D + h_idx * quarter, quarter)
    weight_quarter = lax.all_gather(patch_weight, "ctx", axis=1, tiled=True)
    block_patches = gather_rows(patches, "head").reshape(-1, patches.shape[1])
    embedded = jnp.dot(block_patches, weight_quarter, preferred_element_type=jnp.float32)
    squares = gather_rows(jnp.sum(embedded * embedded, -1), "head")
    inverse = lax.rsqrt(jnp.sum(squares, 0) / D + 1e-06)[:, None]
    normed_quarter = (embedded * inverse * (1.0 + scale) + shift).astype(jnp.bfloat16)
    normed = lax.all_gather(normed_quarter, "head", axis=1, tiled=True)
    group_rows = normed.shape[0]
    heads_here = qkv_weight.shape[1]
    out_cols = heads_here * 3 * HDIM
    local = qkv_weight.reshape(qkv_weight.shape[0], out_cols)
    rows = local.shape[0]
    half_rows = rows // 2
    quarter_rows = half_rows // 2
    core = lax.axis_index("dp") % 2
    mine = lax.dynamic_slice_in_dim(local, core * half_rows, half_rows, 0)
    n_dp = lax.axis_size("dp")

    def send(cells, step):
        return lax.ppermute(cells, "ctx", [(i, step(i)) for i in range(n_ctx)])

    def swap(cells):
        return lax.ppermute(cells, "dp", [(i, i ^ 1) for i in range(n_dp)])

    up = lambda i: (i + 2) % n_ctx
    down = lambda i: (i + n_ctx - 2) % n_ctx
    across = lambda i: i ^ 1
    from_up = (c_idx + n_ctx - 2) % n_ctx
    from_down = (c_idx + 2) % n_ctx
    opposite = (c_idx + 4) % n_ctx
    a_up = send(mine, up)
    a_down = send(mine, down)
    a_across = send(mine, across)
    b_up = send(a_up[:quarter_rows], up)
    b_down = send(a_down[quarter_rows:], down)
    b_across_up = send(a_across, up)
    b_across_down = send(a_across, down)
    c_first = send(b_up, across)
    c_second = send(b_down, across)
    stages = [
        [(a_up, from_up, 0), (a_down, from_down, 0), (a_across, c_idx ^ 1, 0)],
        [(b_up, opposite, 0), (b_down, opposite, quarter_rows),
         (b_across_up, from_up ^ 1, 0), (b_across_down, from_down ^ 1, 0)],
        [(c_first, opposite ^ 1, 0), (c_second, opposite ^ 1, quarter_rows)],
    ]
    qkv = None
    for number, stage in enumerate(stages):
        weights = [local] if number == 0 else []
        columns = [lax.dynamic_slice_in_dim(normed, c_idx * rows, rows, 1)] if number == 0 else []
        for cells, block, offset in stage:
            for side, held in ((core, cells), (1 - core, swap(cells))):
                weights.append(held)
                columns.append(
                    lax.dynamic_slice_in_dim(
                        normed, block * rows + side * half_rows + offset, held.shape[0], 1
                    )
                )
        part = jnp.dot(
            jnp.concatenate(columns, 1),
            jnp.concatenate(weights, 0),
            preferred_element_type=jnp.float32,
        )
        qkv = part if qkv is None else qkv + part
    qkv = qkv.astype(jnp.bfloat16).reshape(group_rows, heads_here, 3, HDIM)
    active = min(heads_here, n_ctx)
    received = [lax.dynamic_index_in_dim(qkv, jnp.minimum(c_idx, active - 1), 1, keepdims=False)]
    for s in range(1, n_ctx):
        target = jnp.minimum((c_idx + s) % n_ctx, active - 1)
        received.append(
            lax.ppermute(
                lax.dynamic_index_in_dim(qkv, target, 1, keepdims=False),
                "ctx",
                [(b, (b + s) % n_ctx) for b in range(n_ctx) if (b + s) % n_ctx < active],
            )
        )
    triple = jnp.stack(received)
    keys = triple[:, :, 1].reshape(-1, HDIM)
    values = triple[:, :, 2].reshape(-1, HDIM)
    inv_root = 1.0 / jnp.sqrt(jnp.float32(HDIM))

    def one_block(query):
        scores = jnp.dot(query, keys.T, preferred_element_type=jnp.float32) * inv_root
        best = jnp.maximum(jnp.float32(-1e30), jnp.max(scores, -1))
        probs = jnp.exp(scores - best[:, None])
        denom = jnp.sum(probs, -1)
        accum = jnp.dot(probs.astype(jnp.bfloat16), values, preferred_element_type=jnp.float32)
        return (accum / denom[:, None]).astype(jnp.bfloat16)

    attended = lax.map(one_block, triple[:, :, 0])
    returned = [attended[0]]
    for s in range(1, n_ctx):
        returned.append(
            lax.ppermute(attended[s], "ctx", [(d, (d - s) % n_ctx) for d in range(active)])
        )
    by_head = jnp.take(jnp.stack(returned), (jnp.arange(heads_here) - c_idx) % n_ctx, axis=0)
    return by_head.transpose(1, 0, 2).reshape(group_rows, heads_here * HDIM)


def solution(mesh):
    return jax.shard_map(
        shards,
        mesh=mesh,
        in_specs=(
            P("dp", "head", "ctx"),
            P("dp", "head", "ctx"),
            P(),
            P(),
            P(),
            P(None, ("head", "ctx")),
            P("dp"),
            P(None, ("head", "ctx")),
            P("ctx", "head", None, None),
        ),
        out_specs=P(("dp", "ctx"), "head"),
        check_vma=False,
    )
```

```python
import jax
import jax.numpy as jnp
from jax import lax
from jax.sharding import PartitionSpec as P

D = 5120
HDIM = 128
FREQ = 256


def with_halo(cells, sides, width):
    for axis, dim in sides:
        count = lax.axis_size(axis)
        ends = count - 1
        head = lax.slice_in_dim(cells, 0, width, axis=dim)
        tail = lax.slice_in_dim(cells, cells.shape[dim] - width, cells.shape[dim], axis=dim)
        cells = jnp.concatenate(
            [
                lax.ppermute(tail, axis, [(i, (i + 1) % count) for i in range(ends)]),
                cells,
                lax.ppermute(head, axis, [((i + 1) % count, i) for i in range(ends)]),
            ],
            axis=dim,
        )
    return cells


def gather_rows(cells, axis):
    count = lax.axis_size(axis)
    me = lax.axis_index(axis)
    parts = [cells] + [
        lax.ppermute(cells, axis, [(i, (i + s) % count) for i in range(count)])
        for s in range(1, count)
    ]
    stacked = jnp.stack(parts)
    return jnp.take(stacked, (me - jnp.arange(count)) % count, axis=0)


def silu_act(value):
    return value * jax.nn.sigmoid(value)


def shards(
    video,
    cache,
    conv_weight,
    conv_bias,
    down_weight,
    patch_weight,
    step_index,
    mod_weight,
    qkv_weight,
):
    cin = conv_weight.shape[2] // 3
    cmid = conv_weight.shape[3]
    frame_count = video.shape[0]
    tile_rows = video.shape[1]
    tile_cols = video.shape[2] // cin
    n_ctx = lax.axis_size("ctx")
    c_idx = lax.axis_index("ctx")
    heads_here = qkv_weight.shape[1]
    out_cols = heads_here * 3 * HDIM
    local = qkv_weight.reshape(qkv_weight.shape[0], out_cols)
    rows = local.shape[0]
    half_rows = rows // 2
    quarter_rows = half_rows // 2
    core = lax.axis_index("dp") % 2
    mine = lax.dynamic_slice_in_dim(local, core * half_rows, half_rows, 0)
    n_dp = lax.axis_size("dp")

    def send(cells, step):
        return lax.ppermute(cells, "ctx", [(i, step(i)) for i in range(n_ctx)])

    def swap(cells):
        return lax.ppermute(cells, "dp", [(i, i ^ 1) for i in range(n_dp)])

    up = lambda i: (i + 2) % n_ctx
    down = lambda i: (i + n_ctx - 2) % n_ctx
    across = lambda i: i ^ 1
    from_up = (c_idx + n_ctx - 2) % n_ctx
    from_down = (c_idx + 2) % n_ctx
    opposite = (c_idx + 4) % n_ctx
    a_up = send(mine, up)
    a_down = send(mine, down)
    a_across = send(mine, across)
    b_up = send(a_up[:quarter_rows], up)
    b_down = send(a_down[quarter_rows:], down)
    b_across_up = send(a_across, up)
    b_across_down = send(a_across, down)
    c_first = send(b_up, across)
    c_second = send(b_down, across)
    stages = [
        [(a_up, from_up, 0), (a_down, from_down, 0), (a_across, c_idx ^ 1, 0)],
        [(b_up, opposite, 0), (b_down, opposite, quarter_rows),
         (b_across_up, from_up ^ 1, 0), (b_across_down, from_down ^ 1, 0)],
        [(c_first, opposite ^ 1, 0), (c_second, opposite ^ 1, quarter_rows)],
    ]
    stages = [[(cells, swap(cells), block, offset) for cells, block, offset in stage] for stage in stages]
    frames = jnp.concatenate([cache, video], 0).reshape(frame_count + 2, tile_rows, tile_cols, cin)
    padded = with_halo(frames, (("head", 1), ("ctx", 2)), 1)
    total = jnp.zeros((frame_count, tile_rows, tile_cols, cmid), jnp.float32)
    for time_tap in range(3):
        for row_tap in range(3):
            slab = padded[time_tap : time_tap + frame_count, row_tap : row_tap + tile_rows]
            stacked = jnp.concatenate(
                [slab[:, :, col_tap : col_tap + tile_cols] for col_tap in range(3)], -1
            )
            total = total + jnp.einsum(
                "fyxc,cd->fyxd",
                stacked,
                conv_weight[time_tap, row_tap],
                preferred_element_type=jnp.float32,
            )
    hidden = silu_act(total + conv_bias).astype(jnp.bfloat16)
    stacked = (
        hidden.reshape(frame_count, tile_rows // 2, 2, tile_cols // 2, 2, cmid)
        .transpose(0, 1, 3, 2, 4, 5)
        .reshape(-1, 4 * cmid)
    )
    reduced = silu_act(jnp.dot(stacked, down_weight, preferred_element_type=jnp.float32)).astype(
        jnp.bfloat16
    )
    reduced = reduced.reshape(frame_count, tile_rows // 2, tile_cols // 2, cmid)
    patches = reduced.reshape(frame_count, tile_rows // 4, 2, tile_cols // 4, 2, cmid).transpose(
        0, 1, 3, 2, 4, 5
    )
    patches = patches.reshape(-1, 4 * cmid)
    patches, stages[0] = lax.optimization_barrier((patches, stages[0]))
    half = FREQ // 2
    freqs = jnp.exp(-jnp.log(10000.0) * jnp.arange(half, dtype=jnp.float32) / half)
    angles = step_index[0].astype(jnp.float32) * freqs
    timing = jnp.concatenate([jnp.cos(angles), jnp.sin(angles)]).astype(jnp.bfloat16)
    mod_share = jnp.dot(timing[None, :], mod_weight, preferred_element_type=jnp.float32)[0]
    modulation = gather_rows(gather_rows(mod_share, "ctx").reshape(-1), "head").reshape(-1)
    n_head = lax.axis_size("head")
    n_ctx = lax.axis_size("ctx")
    h_idx = lax.axis_index("head")
    c_idx = lax.axis_index("ctx")
    quarter = D // n_head
    scale = lax.dynamic_slice_in_dim(modulation, h_idx * quarter, quarter)
    shift = lax.dynamic_slice_in_dim(modulation, D + h_idx * quarter, quarter)
    weight_quarter = lax.all_gather(patch_weight, "ctx", axis=1, tiled=True)
    block_patches = gather_rows(patches, "head").reshape(-1, patches.shape[1])
    embedded = jnp.dot(block_patches, weight_quarter, preferred_element_type=jnp.float32)
    embedded, stages[1] = lax.optimization_barrier((embedded, stages[1]))
    squares = gather_rows(jnp.sum(embedded * embedded, -1), "head")
    inverse = lax.rsqrt(jnp.sum(squares, 0) / D + 1e-06)[:, None]
    normed_quarter = (embedded * inverse * (1.0 + scale) + shift).astype(jnp.bfloat16)
    normed_quarter, stages[2] = lax.optimization_barrier((normed_quarter, stages[2]))
    normed = lax.all_gather(normed_quarter, "head", axis=1, tiled=True)
    group_rows = normed.shape[0]
    heads_here = qkv_weight.shape[1]
    out_cols = heads_here * 3 * HDIM
    qkv = None
    for number, stage in enumerate(stages):
        weights = [local] if number == 0 else []
        columns = [lax.dynamic_slice_in_dim(normed, c_idx * rows, rows, 1)] if number == 0 else []
        for cells, partner, block, offset in stage:
            for side, held in ((core, cells), (1 - core, partner)):
                weights.append(held)
                columns.append(
                    lax.dynamic_slice_in_dim(
                        normed, block * rows + side * half_rows + offset, held.shape[0], 1
                    )
                )
        part = jnp.dot(
            jnp.concatenate(columns, 1),
            jnp.concatenate(weights, 0),
            preferred_element_type=jnp.float32,
        )
        qkv = part if qkv is None else qkv + part
    qkv = qkv.astype(jnp.bfloat16).reshape(group_rows, heads_here, 3, HDIM)
    active = min(heads_here, n_ctx)
    received = [lax.dynamic_index_in_dim(qkv, jnp.minimum(c_idx, active - 1), 1, keepdims=False)]
    for s in range(1, n_ctx):
        target = jnp.minimum((c_idx + s) % n_ctx, active - 1)
        received.append(
            lax.ppermute(
                lax.dynamic_index_in_dim(qkv, target, 1, keepdims=False),
                "ctx",
                [(b, (b + s) % n_ctx) for b in range(n_ctx) if (b + s) % n_ctx < active],
            )
        )
    triple = jnp.stack(received)
    keys = triple[:, :, 1].reshape(-1, HDIM)
    values = triple[:, :, 2].reshape(-1, HDIM)
    inv_root = 1.0 / jnp.sqrt(jnp.float32(HDIM))

    def one_block(query):
        scores = jnp.dot(query, keys.T, preferred_element_type=jnp.float32) * inv_root
        best = jnp.maximum(jnp.float32(-1e30), jnp.max(scores, -1))
        probs = jnp.exp(scores - best[:, None])
        denom = jnp.sum(probs, -1)
        accum = jnp.dot(probs.astype(jnp.bfloat16), values, preferred_element_type=jnp.float32)
        return (accum / denom[:, None]).astype(jnp.bfloat16)

    attended = lax.map(one_block, triple[:, :, 0])
    returned = [attended[0]]
    for s in range(1, n_ctx):
        returned.append(
            lax.ppermute(attended[s], "ctx", [(d, (d - s) % n_ctx) for d in range(active)])
        )
    by_head = jnp.take(jnp.stack(returned), (jnp.arange(heads_here) - c_idx) % n_ctx, axis=0)
    return by_head.transpose(1, 0, 2).reshape(group_rows, heads_here * HDIM)


def solution(mesh):
    return jax.shard_map(
        shards,
        mesh=mesh,
        in_specs=(
            P("dp", "head", "ctx"),
            P("dp", "head", "ctx"),
            P(),
            P(),
            P(),
            P(None, ("head", "ctx")),
            P("dp"),
            P(None, ("head", "ctx")),
            P("ctx", "head", None, None),
        ),
        out_specs=P(("dp", "ctx"), "head"),
        check_vma=False,
    )
```

```python
import jax
import jax.numpy as jnp
from jax import lax
from jax.sharding import PartitionSpec as P

D = 5120
HDIM = 128
FREQ = 256


def with_halo(cells, sides, width):
    for axis, dim in sides:
        count = lax.axis_size(axis)
        ends = count - 1
        head = lax.slice_in_dim(cells, 0, width, axis=dim)
        tail = lax.slice_in_dim(cells, cells.shape[dim] - width, cells.shape[dim], axis=dim)
        cells = jnp.concatenate(
            [
                lax.ppermute(tail, axis, [(i, (i + 1) % count) for i in range(ends)]),
                cells,
                lax.ppermute(head, axis, [((i + 1) % count, i) for i in range(ends)]),
            ],
            axis=dim,
        )
    return cells


def gather_rows(cells, axis):
    count = lax.axis_size(axis)
    me = lax.axis_index(axis)
    parts = [cells] + [
        lax.ppermute(cells, axis, [(i, (i + s) % count) for i in range(count)])
        for s in range(1, count)
    ]
    stacked = jnp.stack(parts)
    return jnp.take(stacked, (me - jnp.arange(count)) % count, axis=0)


def split3(value):
    parts = []
    rest = value
    for _ in range(3):
        part = lax.reduce_precision(rest, exponent_bits=8, mantissa_bits=7)
        parts.append(part.astype(jnp.bfloat16))
        rest = rest - part
    return jnp.stack(parts)


def join3(parts):
    return (parts[0].astype(jnp.float32) + parts[1].astype(jnp.float32)) + parts[2].astype(jnp.float32)


def silu_act(value):
    return value * jax.nn.sigmoid(value)


def shards(
    video,
    cache,
    conv_weight,
    conv_bias,
    down_weight,
    patch_weight,
    step_index,
    mod_weight,
    qkv_weight,
):
    cin = conv_weight.shape[2] // 3
    cmid = conv_weight.shape[3]
    frame_count = video.shape[0]
    tile_rows = video.shape[1]
    tile_cols = video.shape[2] // cin
    frames = jnp.concatenate([cache, video], 0).reshape(frame_count + 2, tile_rows, tile_cols, cin)
    padded = with_halo(frames, (("head", 1), ("ctx", 2)), 1)
    total = jnp.zeros((frame_count, tile_rows, tile_cols, cmid), jnp.float32)
    for time_tap in range(3):
        for row_tap in range(3):
            slab = padded[time_tap : time_tap + frame_count, row_tap : row_tap + tile_rows]
            stacked = jnp.concatenate(
                [slab[:, :, col_tap : col_tap + tile_cols] for col_tap in range(3)], -1
            )
            total = total + jnp.einsum(
                "fyxc,cd->fyxd",
                stacked,
                conv_weight[time_tap, row_tap],
                preferred_element_type=jnp.float32,
            )
    hidden = silu_act(total + conv_bias).astype(jnp.bfloat16)
    stacked = (
        hidden.reshape(frame_count, tile_rows // 2, 2, tile_cols // 2, 2, cmid)
        .transpose(0, 1, 3, 2, 4, 5)
        .reshape(-1, 4 * cmid)
    )
    reduced = silu_act(jnp.dot(stacked, down_weight, preferred_element_type=jnp.float32)).astype(
        jnp.bfloat16
    )
    reduced = reduced.reshape(frame_count, tile_rows // 2, tile_cols // 2, cmid)
    patches = reduced.reshape(frame_count, tile_rows // 4, 2, tile_cols // 4, 2, cmid).transpose(
        0, 1, 3, 2, 4, 5
    )
    patches = patches.reshape(-1, 4 * cmid)
    half = FREQ // 2
    freqs = jnp.exp(-jnp.log(10000.0) * jnp.arange(half, dtype=jnp.float32) / half)
    angles = step_index[0].astype(jnp.float32) * freqs
    timing = jnp.concatenate([jnp.cos(angles), jnp.sin(angles)]).astype(jnp.bfloat16)
    mod_share = jnp.dot(timing[None, :], mod_weight, preferred_element_type=jnp.float32)[0]
    n_head = lax.axis_size("head")
    n_ctx = lax.axis_size("ctx")
    h_idx = lax.axis_index("head")
    c_idx = lax.axis_index("ctx")
    quarter = D // n_head
    share_width = patch_weight.shape[1]
    share_parts = split3(mod_share).reshape(-1, share_width)
    carried = lax.all_gather(
        jnp.concatenate([patch_weight, share_parts], 0), "ctx", axis=1, tiled=True
    )
    weight_quarter = carried[: patch_weight.shape[0]]
    row_share = (
        carried[patch_weight.shape[0] :]
        .reshape(-1, n_ctx, share_width)
        .transpose(1, 0, 2)
        .reshape(n_ctx, 3, -1)
        .transpose(1, 0, 2)
        .reshape(3, -1)
    )
    row_parts = join3(row_share)
    token_width = patches.shape[1]
    riding = jnp.concatenate([patches, split3(row_parts).reshape(-1, token_width)], 0)
    gathered_rows = gather_rows(riding, "head")
    block_patches = gathered_rows[:, : patches.shape[0]].reshape(-1, token_width)
    modulation = join3(
        gathered_rows[:, patches.shape[0] :].reshape(n_head, 3, -1).transpose(1, 0, 2).reshape(3, -1)
    )
    scale = lax.dynamic_slice_in_dim(modulation, h_idx * quarter, quarter)
    shift = lax.dynamic_slice_in_dim(modulation, D + h_idx * quarter, quarter)
    embedded = jnp.dot(block_patches, weight_quarter, preferred_element_type=jnp.float32)
    squares = gather_rows(jnp.sum(embedded * embedded, -1), "head")
    inverse = lax.rsqrt(jnp.sum(squares, 0) / D + 1e-06)[:, None]
    normed_quarter = (embedded * inverse * (1.0 + scale) + shift).astype(jnp.bfloat16)
    normed = lax.all_gather(normed_quarter, "head", axis=1, tiled=True)
    group_rows = normed.shape[0]
    heads_here = qkv_weight.shape[1]
    out_cols = heads_here * 3 * HDIM
    local = qkv_weight.reshape(qkv_weight.shape[0], out_cols)
    rows = local.shape[0]
    half_rows = rows // 2
    quarter_rows = half_rows // 2
    core = lax.axis_index("dp") % 2
    mine = lax.dynamic_slice_in_dim(local, core * half_rows, half_rows, 0)
    n_dp = lax.axis_size("dp")

    def send(cells, step):
        return lax.ppermute(cells, "ctx", [(i, step(i)) for i in range(n_ctx)])

    def swap(cells):
        return lax.ppermute(cells, "dp", [(i, i ^ 1) for i in range(n_dp)])

    up = lambda i: (i + 2) % n_ctx
    down = lambda i: (i + n_ctx - 2) % n_ctx
    across = lambda i: i ^ 1
    from_up = (c_idx + n_ctx - 2) % n_ctx
    from_down = (c_idx + 2) % n_ctx
    opposite = (c_idx + 4) % n_ctx
    a_up = send(mine, up)
    a_down = send(mine, down)
    a_across = send(mine, across)
    b_up = send(a_up[:quarter_rows], up)
    b_down = send(a_down[quarter_rows:], down)
    b_across_up = send(a_across, up)
    b_across_down = send(a_across, down)
    c_first = send(b_up, across)
    c_second = send(b_down, across)
    stages = [
        [(a_up, from_up, 0), (a_down, from_down, 0), (a_across, c_idx ^ 1, 0)],
        [(b_up, opposite, 0), (b_down, opposite, quarter_rows),
         (b_across_up, from_up ^ 1, 0), (b_across_down, from_down ^ 1, 0)],
        [(c_first, opposite ^ 1, 0), (c_second, opposite ^ 1, quarter_rows)],
    ]
    qkv = None
    for number, stage in enumerate(stages):
        weights = [local] if number == 0 else []
        columns = [lax.dynamic_slice_in_dim(normed, c_idx * rows, rows, 1)] if number == 0 else []
        ours = jnp.concatenate([cells for cells, _, _ in stage], 0)
        weights += [ours, swap(ours)]
        for side in (core, 1 - core):
            for cells, block, offset in stage:
                columns.append(
                    lax.dynamic_slice_in_dim(
                        normed, block * rows + side * half_rows + offset, cells.shape[0], 1
                    )
                )
        part = jnp.dot(
            jnp.concatenate(columns, 1),
            jnp.concatenate(weights, 0),
            preferred_element_type=jnp.float32,
        )
        qkv = part if qkv is None else qkv + part
    qkv = qkv.astype(jnp.bfloat16).reshape(group_rows, heads_here, 3, HDIM)
    active = min(heads_here, n_ctx)
    received = [lax.dynamic_index_in_dim(qkv, jnp.minimum(c_idx, active - 1), 1, keepdims=False)]
    for s in range(1, n_ctx):
        target = jnp.minimum((c_idx + s) % n_ctx, active - 1)
        received.append(
            lax.ppermute(
                lax.dynamic_index_in_dim(qkv, target, 1, keepdims=False),
                "ctx",
                [(b, (b + s) % n_ctx) for b in range(n_ctx) if (b + s) % n_ctx < active],
            )
        )
    triple = jnp.stack(received)
    keys = triple[:, :, 1].reshape(-1, HDIM)
    values = triple[:, :, 2].reshape(-1, HDIM)
    inv_root = 1.0 / jnp.sqrt(jnp.float32(HDIM))

    def one_block(query):
        scores = jnp.dot(query, keys.T, preferred_element_type=jnp.float32) * inv_root
        best = jnp.maximum(jnp.float32(-1e30), jnp.max(scores, -1))
        probs = jnp.exp(scores - best[:, None])
        denom = jnp.sum(probs, -1)
        accum = jnp.dot(probs.astype(jnp.bfloat16), values, preferred_element_type=jnp.float32)
        return (accum / denom[:, None]).astype(jnp.bfloat16)

    attended = lax.map(one_block, triple[:, :, 0])
    returned = [attended[0]]
    for s in range(1, n_ctx):
        returned.append(
            lax.ppermute(attended[s], "ctx", [(d, (d - s) % n_ctx) for d in range(active)])
        )
    by_head = jnp.take(jnp.stack(returned), (jnp.arange(heads_here) - c_idx) % n_ctx, axis=0)
    return by_head.transpose(1, 0, 2).reshape(group_rows, heads_here * HDIM)


def solution(mesh):
    return jax.shard_map(
        shards,
        mesh=mesh,
        in_specs=(
            P("dp", "head", "ctx"),
            P("dp", "head", "ctx"),
            P(),
            P(),
            P(),
            P(None, ("head", "ctx")),
            P("dp"),
            P(None, ("head", "ctx")),
            P("ctx", "head", None, None),
        ),
        out_specs=P(("dp", "ctx"), "head"),
        check_vma=False,
    )
```

```python
import jax
import jax.numpy as jnp
from jax import lax
from jax.sharding import PartitionSpec as P

D = 5120
HDIM = 128
FREQ = 256


def with_halo(cells, sides, width):
    for axis, dim in sides:
        count = lax.axis_size(axis)
        ends = count - 1
        head = lax.slice_in_dim(cells, 0, width, axis=dim)
        tail = lax.slice_in_dim(cells, cells.shape[dim] - width, cells.shape[dim], axis=dim)
        cells = jnp.concatenate(
            [
                lax.ppermute(tail, axis, [(i, (i + 1) % count) for i in range(ends)]),
                cells,
                lax.ppermute(head, axis, [((i + 1) % count, i) for i in range(ends)]),
            ],
            axis=dim,
        )
    return cells


def gather_rows(cells, axis):
    count = lax.axis_size(axis)
    me = lax.axis_index(axis)
    parts = [cells] + [
        lax.ppermute(cells, axis, [(i, (i + s) % count) for i in range(count)])
        for s in range(1, count)
    ]
    stacked = jnp.stack(parts)
    return jnp.take(stacked, (me - jnp.arange(count)) % count, axis=0)


def split3(value):
    parts = []
    rest = value
    for _ in range(3):
        part = lax.reduce_precision(rest, exponent_bits=8, mantissa_bits=7)
        parts.append(part.astype(jnp.bfloat16))
        rest = rest - part
    return jnp.stack(parts)


def join3(parts):
    return (parts[0].astype(jnp.float32) + parts[1].astype(jnp.float32)) + parts[2].astype(jnp.float32)


def silu_act(value):
    return value * jax.nn.sigmoid(value)


def shards(
    video,
    cache,
    conv_weight,
    conv_bias,
    down_weight,
    patch_weight,
    step_index,
    mod_weight,
    qkv_weight,
):
    cin = conv_weight.shape[2] // 3
    cmid = conv_weight.shape[3]
    frame_count = video.shape[0]
    tile_rows = video.shape[1]
    tile_cols = video.shape[2] // cin
    n_ctx = lax.axis_size("ctx")
    c_idx = lax.axis_index("ctx")
    heads_here = qkv_weight.shape[1]
    out_cols = heads_here * 3 * HDIM
    local = qkv_weight.reshape(qkv_weight.shape[0], out_cols)
    rows = local.shape[0]
    half_rows = rows // 2
    quarter_rows = half_rows // 2
    core = lax.axis_index("dp") % 2
    mine = lax.dynamic_slice_in_dim(local, core * half_rows, half_rows, 0)
    n_dp = lax.axis_size("dp")

    def send(cells, step):
        return lax.ppermute(cells, "ctx", [(i, step(i)) for i in range(n_ctx)])

    def swap(cells):
        return lax.ppermute(cells, "dp", [(i, i ^ 1) for i in range(n_dp)])

    up = lambda i: (i + 2) % n_ctx
    down = lambda i: (i + n_ctx - 2) % n_ctx
    across = lambda i: i ^ 1
    from_up = (c_idx + n_ctx - 2) % n_ctx
    from_down = (c_idx + 2) % n_ctx
    opposite = (c_idx + 4) % n_ctx
    a_up = send(mine, up)
    a_down = send(mine, down)
    a_across = send(mine, across)
    b_up = send(a_up[:quarter_rows], up)
    b_down = send(a_down[quarter_rows:], down)
    b_across_up = send(a_across, up)
    b_across_down = send(a_across, down)
    c_first = send(b_up, across)
    c_second = send(b_down, across)
    stages = [
        [(a_up, from_up, 0), (a_down, from_down, 0), (a_across, c_idx ^ 1, 0)],
        [(b_up, opposite, 0), (b_down, opposite, quarter_rows),
         (b_across_up, from_up ^ 1, 0), (b_across_down, from_down ^ 1, 0)],
        [(c_first, opposite ^ 1, 0), (c_second, opposite ^ 1, quarter_rows)],
    ]
    stages = [
        (stage, ours, swap(ours))
        for stage, ours in ((s, jnp.concatenate([cells for cells, _, _ in s], 0)) for s in stages)
    ]
    frames = jnp.concatenate([cache, video], 0).reshape(frame_count + 2, tile_rows, tile_cols, cin)
    padded = with_halo(frames, (("head", 1), ("ctx", 2)), 1)
    total = jnp.zeros((frame_count, tile_rows, tile_cols, cmid), jnp.float32)
    for time_tap in range(3):
        for row_tap in range(3):
            slab = padded[time_tap : time_tap + frame_count, row_tap : row_tap + tile_rows]
            stacked = jnp.concatenate(
                [slab[:, :, col_tap : col_tap + tile_cols] for col_tap in range(3)], -1
            )
            total = total + jnp.einsum(
                "fyxc,cd->fyxd",
                stacked,
                conv_weight[time_tap, row_tap],
                preferred_element_type=jnp.float32,
            )
    hidden = silu_act(total + conv_bias).astype(jnp.bfloat16)
    stacked = (
        hidden.reshape(frame_count, tile_rows // 2, 2, tile_cols // 2, 2, cmid)
        .transpose(0, 1, 3, 2, 4, 5)
        .reshape(-1, 4 * cmid)
    )
    reduced = silu_act(jnp.dot(stacked, down_weight, preferred_element_type=jnp.float32)).astype(
        jnp.bfloat16
    )
    reduced = reduced.reshape(frame_count, tile_rows // 2, tile_cols // 2, cmid)
    patches = reduced.reshape(frame_count, tile_rows // 4, 2, tile_cols // 4, 2, cmid).transpose(
        0, 1, 3, 2, 4, 5
    )
    patches = patches.reshape(-1, 4 * cmid)
    patches, stages[0] = lax.optimization_barrier((patches, stages[0]))
    half = FREQ // 2
    freqs = jnp.exp(-jnp.log(10000.0) * jnp.arange(half, dtype=jnp.float32) / half)
    angles = step_index[0].astype(jnp.float32) * freqs
    timing = jnp.concatenate([jnp.cos(angles), jnp.sin(angles)]).astype(jnp.bfloat16)
    mod_share = jnp.dot(timing[None, :], mod_weight, preferred_element_type=jnp.float32)[0]
    n_head = lax.axis_size("head")
    n_ctx = lax.axis_size("ctx")
    h_idx = lax.axis_index("head")
    c_idx = lax.axis_index("ctx")
    quarter = D // n_head
    share_width = patch_weight.shape[1]
    share_parts = split3(mod_share).reshape(-1, share_width)
    carried = lax.all_gather(
        jnp.concatenate([patch_weight, share_parts], 0), "ctx", axis=1, tiled=True
    )
    weight_quarter = carried[: patch_weight.shape[0]]
    row_share = (
        carried[patch_weight.shape[0] :]
        .reshape(-1, n_ctx, share_width)
        .transpose(1, 0, 2)
        .reshape(n_ctx, 3, -1)
        .transpose(1, 0, 2)
        .reshape(3, -1)
    )
    row_parts = join3(row_share)
    block_patches = gather_rows(patches, "head").reshape(-1, patches.shape[1])
    embedded = jnp.dot(block_patches, weight_quarter, preferred_element_type=jnp.float32)
    embedded, stages[1] = lax.optimization_barrier((embedded, stages[1]))
    token_count = embedded.shape[0]
    riding = gather_rows(jnp.concatenate([jnp.sum(embedded * embedded, -1), row_parts]), "head")
    squares = riding[:, :token_count]
    modulation = riding[:, token_count:].reshape(-1)
    scale = lax.dynamic_slice_in_dim(modulation, h_idx * quarter, quarter)
    shift = lax.dynamic_slice_in_dim(modulation, D + h_idx * quarter, quarter)
    inverse = lax.rsqrt(jnp.sum(squares, 0) / D + 1e-06)[:, None]
    normed_quarter = (embedded * inverse * (1.0 + scale) + shift).astype(jnp.bfloat16)
    normed = lax.all_gather(normed_quarter, "head", axis=1, tiled=True)
    group_rows = normed.shape[0]
    heads_here = qkv_weight.shape[1]
    out_cols = heads_here * 3 * HDIM
    qkv = None
    for number, (stage, ours, theirs) in enumerate(stages):
        weights = [local] if number == 0 else []
        columns = [lax.dynamic_slice_in_dim(normed, c_idx * rows, rows, 1)] if number == 0 else []
        weights += [ours, theirs]
        for side in (core, 1 - core):
            for cells, block, offset in stage:
                columns.append(
                    lax.dynamic_slice_in_dim(
                        normed, block * rows + side * half_rows + offset, cells.shape[0], 1
                    )
                )
        part = jnp.dot(
            jnp.concatenate(columns, 1),
            jnp.concatenate(weights, 0),
            preferred_element_type=jnp.float32,
        )
        qkv = part if qkv is None else qkv + part
    qkv = qkv.astype(jnp.bfloat16).reshape(group_rows, heads_here, 3, HDIM)
    active = min(heads_here, n_ctx)
    received = [lax.dynamic_index_in_dim(qkv, jnp.minimum(c_idx, active - 1), 1, keepdims=False)]
    for s in range(1, n_ctx):
        target = jnp.minimum((c_idx + s) % n_ctx, active - 1)
        received.append(
            lax.ppermute(
                lax.dynamic_index_in_dim(qkv, target, 1, keepdims=False),
                "ctx",
                [(b, (b + s) % n_ctx) for b in range(n_ctx) if (b + s) % n_ctx < active],
            )
        )
    triple = jnp.stack(received)
    keys = triple[:, :, 1].reshape(-1, HDIM)
    values = triple[:, :, 2].reshape(-1, HDIM)
    inv_root = 1.0 / jnp.sqrt(jnp.float32(HDIM))

    def one_block(query):
        scores = jnp.dot(query, keys.T, preferred_element_type=jnp.float32) * inv_root
        best = jnp.maximum(jnp.float32(-1e30), jnp.max(scores, -1))
        probs = jnp.exp(scores - best[:, None])
        denom = jnp.sum(probs, -1)
        accum = jnp.dot(probs.astype(jnp.bfloat16), values, preferred_element_type=jnp.float32)
        return (accum / denom[:, None]).astype(jnp.bfloat16)

    attended = lax.map(one_block, triple[:, :, 0])
    returned = [attended[0]]
    for s in range(1, n_ctx):
        returned.append(
            lax.ppermute(attended[s], "ctx", [(d, (d - s) % n_ctx) for d in range(active)])
        )
    by_head = jnp.take(jnp.stack(returned), (jnp.arange(heads_here) - c_idx) % n_ctx, axis=0)
    return by_head.transpose(1, 0, 2).reshape(group_rows, heads_here * HDIM)


def solution(mesh):
    return jax.shard_map(
        shards,
        mesh=mesh,
        in_specs=(
            P("dp", "head", "ctx"),
            P("dp", "head", "ctx"),
            P(),
            P(),
            P(),
            P(None, ("head", "ctx")),
            P("dp"),
            P(None, ("head", "ctx")),
            P("ctx", "head", None, None),
        ),
        out_specs=P(("dp", "ctx"), "head"),
        check_vma=False,
    )
```

```python
import jax
import jax.numpy as jnp
from jax import lax
from jax.sharding import PartitionSpec as P

D = 5120
HDIM = 128
FREQ = 256


def with_halo(cells, sides, width):
    for axis, dim in sides:
        count = lax.axis_size(axis)
        ends = count - 1
        head = lax.slice_in_dim(cells, 0, width, axis=dim)
        tail = lax.slice_in_dim(cells, cells.shape[dim] - width, cells.shape[dim], axis=dim)
        cells = jnp.concatenate(
            [
                lax.ppermute(tail, axis, [(i, (i + 1) % count) for i in range(ends)]),
                cells,
                lax.ppermute(head, axis, [((i + 1) % count, i) for i in range(ends)]),
            ],
            axis=dim,
        )
    return cells


def gather_rows(cells, axis):
    count = lax.axis_size(axis)
    me = lax.axis_index(axis)
    parts = [cells] + [
        lax.ppermute(cells, axis, [(i, (i + s) % count) for i in range(count)])
        for s in range(1, count)
    ]
    stacked = jnp.stack(parts)
    return jnp.take(stacked, (me - jnp.arange(count)) % count, axis=0)


def split3(value):
    parts = []
    rest = value
    for _ in range(3):
        part = lax.reduce_precision(rest, exponent_bits=8, mantissa_bits=7)
        parts.append(part.astype(jnp.bfloat16))
        rest = rest - part
    return jnp.stack(parts)


def join3(parts):
    return (parts[0].astype(jnp.float32) + parts[1].astype(jnp.float32)) + parts[2].astype(jnp.float32)


def silu_act(value):
    return value * jax.nn.sigmoid(value)


def shards(
    video,
    cache,
    conv_weight,
    conv_bias,
    down_weight,
    patch_weight,
    step_index,
    mod_weight,
    qkv_weight,
):
    cin = conv_weight.shape[2] // 3
    cmid = conv_weight.shape[3]
    frame_count = video.shape[0]
    tile_rows = video.shape[1]
    tile_cols = video.shape[2] // cin
    n_ctx = lax.axis_size("ctx")
    c_idx = lax.axis_index("ctx")
    heads_here = qkv_weight.shape[1]
    out_cols = heads_here * 3 * HDIM
    local = qkv_weight.reshape(qkv_weight.shape[0], out_cols)
    rows = local.shape[0]
    half_rows = rows // 2
    quarter_rows = half_rows // 2
    core = lax.axis_index("dp") % 2
    mine = lax.dynamic_slice_in_dim(local, core * half_rows, half_rows, 0)
    n_dp = lax.axis_size("dp")

    def send(cells, step):
        return lax.ppermute(cells, "ctx", [(i, step(i)) for i in range(n_ctx)])

    def swap(cells):
        return lax.ppermute(cells, "dp", [(i, i ^ 1) for i in range(n_dp)])

    up = lambda i: (i + 2) % n_ctx
    down = lambda i: (i + n_ctx - 2) % n_ctx
    across = lambda i: i ^ 1
    from_up = (c_idx + n_ctx - 2) % n_ctx
    from_down = (c_idx + 2) % n_ctx
    opposite = (c_idx + 4) % n_ctx
    a_up = send(mine, up)
    a_down = send(mine, down)
    a_across = send(mine, across)
    b_up = send(a_up[:quarter_rows], up)
    b_down = send(a_down[quarter_rows:], down)
    b_across_up = send(a_across, up)
    b_across_down = send(a_across, down)
    c_first = send(b_up, across)
    c_second = send(b_down, across)
    stages = [
        [(a_up, from_up, 0), (a_down, from_down, 0), (a_across, c_idx ^ 1, 0)],
        [(b_up, opposite, 0), (b_down, opposite, quarter_rows),
         (b_across_up, from_up ^ 1, 0), (b_across_down, from_down ^ 1, 0)],
        [(c_first, opposite ^ 1, 0), (c_second, opposite ^ 1, quarter_rows)],
    ]
    stages = [
        (stage, ours, swap(ours))
        for stage, ours in ((s, jnp.concatenate([cells for cells, _, _ in s], 0)) for s in stages)
    ]
    frames = jnp.concatenate([cache, video], 0).reshape(frame_count + 2, tile_rows, tile_cols, cin)
    padded = with_halo(frames, (("head", 1), ("ctx", 2)), 1)
    total = jnp.zeros((frame_count, tile_rows, tile_cols, cmid), jnp.float32)
    for time_tap in range(3):
        for row_tap in range(3):
            slab = padded[time_tap : time_tap + frame_count, row_tap : row_tap + tile_rows]
            stacked = jnp.concatenate(
                [slab[:, :, col_tap : col_tap + tile_cols] for col_tap in range(3)], -1
            )
            total = total + jnp.einsum(
                "fyxc,cd->fyxd",
                stacked,
                conv_weight[time_tap, row_tap],
                preferred_element_type=jnp.float32,
            )
    hidden = silu_act(total + conv_bias).astype(jnp.bfloat16)
    stacked = (
        hidden.reshape(frame_count, tile_rows // 2, 2, tile_cols // 2, 2, cmid)
        .transpose(0, 1, 3, 2, 4, 5)
        .reshape(-1, 4 * cmid)
    )
    reduced = silu_act(jnp.dot(stacked, down_weight, preferred_element_type=jnp.float32)).astype(
        jnp.bfloat16
    )
    reduced = reduced.reshape(frame_count, tile_rows // 2, tile_cols // 2, cmid)
    patches = reduced.reshape(frame_count, tile_rows // 4, 2, tile_cols // 4, 2, cmid).transpose(
        0, 1, 3, 2, 4, 5
    )
    patches = patches.reshape(-1, 4 * cmid)
    half = FREQ // 2
    freqs = jnp.exp(-jnp.log(10000.0) * jnp.arange(half, dtype=jnp.float32) / half)
    angles = step_index[0].astype(jnp.float32) * freqs
    timing = jnp.concatenate([jnp.cos(angles), jnp.sin(angles)]).astype(jnp.bfloat16)
    mod_share = jnp.dot(timing[None, :], mod_weight, preferred_element_type=jnp.float32)[0]
    n_head = lax.axis_size("head")
    n_ctx = lax.axis_size("ctx")
    h_idx = lax.axis_index("head")
    c_idx = lax.axis_index("ctx")
    quarter = D // n_head
    share_width = patch_weight.shape[1]
    share_parts = split3(mod_share).reshape(-1, share_width)
    carried = lax.all_gather(
        jnp.concatenate([patch_weight, share_parts], 0), "ctx", axis=1, tiled=True
    )
    weight_quarter = carried[: patch_weight.shape[0]]
    row_share = (
        carried[patch_weight.shape[0] :]
        .reshape(-1, n_ctx, share_width)
        .transpose(1, 0, 2)
        .reshape(n_ctx, 3, -1)
        .transpose(1, 0, 2)
        .reshape(3, -1)
    )
    row_parts = join3(row_share)
    block_patches = gather_rows(patches, "head").reshape(-1, patches.shape[1])
    embedded = jnp.dot(block_patches, weight_quarter, preferred_element_type=jnp.float32)
    token_count = embedded.shape[0]
    riding = gather_rows(jnp.concatenate([jnp.sum(embedded * embedded, -1), row_parts]), "head")
    squares = riding[:, :token_count]
    modulation = riding[:, token_count:].reshape(-1)
    scale = lax.dynamic_slice_in_dim(modulation, h_idx * quarter, quarter)
    shift = lax.dynamic_slice_in_dim(modulation, D + h_idx * quarter, quarter)
    inverse = lax.rsqrt(jnp.sum(squares, 0) / D + 1e-06)[:, None]
    normed_quarter = (embedded * inverse * (1.0 + scale) + shift).astype(jnp.bfloat16)
    normed = lax.all_gather(normed_quarter, "head", axis=1, tiled=True)
    group_rows = normed.shape[0]
    heads_here = qkv_weight.shape[1]
    out_cols = heads_here * 3 * HDIM
    qkv = None
    for number, (stage, ours, theirs) in enumerate(stages):
        weights = [local] if number == 0 else []
        columns = [lax.dynamic_slice_in_dim(normed, c_idx * rows, rows, 1)] if number == 0 else []
        weights += [ours, theirs]
        for side in (core, 1 - core):
            for cells, block, offset in stage:
                columns.append(
                    lax.dynamic_slice_in_dim(
                        normed, block * rows + side * half_rows + offset, cells.shape[0], 1
                    )
                )
        part = jnp.dot(
            jnp.concatenate(columns, 1),
            jnp.concatenate(weights, 0),
            preferred_element_type=jnp.float32,
        )
        qkv = part if qkv is None else qkv + part
    qkv = qkv.astype(jnp.bfloat16).reshape(group_rows, heads_here, 3, HDIM)
    active = min(heads_here, n_ctx)
    received = [lax.dynamic_index_in_dim(qkv, jnp.minimum(c_idx, active - 1), 1, keepdims=False)]
    for s in range(1, n_ctx):
        target = jnp.minimum((c_idx + s) % n_ctx, active - 1)
        received.append(
            lax.ppermute(
                lax.dynamic_index_in_dim(qkv, target, 1, keepdims=False),
                "ctx",
                [(b, (b + s) % n_ctx) for b in range(n_ctx) if (b + s) % n_ctx < active],
            )
        )
    triple = jnp.stack(received)
    keys = triple[:, :, 1].reshape(-1, HDIM)
    values = triple[:, :, 2].reshape(-1, HDIM)
    inv_root = 1.0 / jnp.sqrt(jnp.float32(HDIM))

    def one_block(query):
        scores = jnp.dot(query, keys.T, preferred_element_type=jnp.float32) * inv_root
        best = jnp.maximum(jnp.float32(-1e30), jnp.max(scores, -1))
        probs = jnp.exp(scores - best[:, None])
        denom = jnp.sum(probs, -1)
        accum = jnp.dot(probs.astype(jnp.bfloat16), values, preferred_element_type=jnp.float32)
        return (accum / denom[:, None]).astype(jnp.bfloat16)

    attended = lax.map(one_block, triple[:, :, 0])
    returned = [attended[0]]
    for s in range(1, n_ctx):
        returned.append(
            lax.ppermute(attended[s], "ctx", [(d, (d - s) % n_ctx) for d in range(active)])
        )
    by_head = jnp.take(jnp.stack(returned), (jnp.arange(heads_here) - c_idx) % n_ctx, axis=0)
    return by_head.transpose(1, 0, 2).reshape(group_rows, heads_here * HDIM)


def solution(mesh):
    return jax.shard_map(
        shards,
        mesh=mesh,
        in_specs=(
            P("dp", "head", "ctx"),
            P("dp", "head", "ctx"),
            P(),
            P(),
            P(),
            P(None, ("head", "ctx")),
            P("dp"),
            P(None, ("head", "ctx")),
            P("ctx", "head", None, None),
        ),
        out_specs=P(("dp", "ctx"), "head"),
        check_vma=False,
    )
```

```python
import jax
import jax.numpy as jnp
from jax import lax
from jax.sharding import PartitionSpec as P

D = 5120
HDIM = 128
FREQ = 256


def with_halo(cells, sides, width):
    for axis, dim in sides:
        count = lax.axis_size(axis)
        ends = count - 1
        head = lax.slice_in_dim(cells, 0, width, axis=dim)
        tail = lax.slice_in_dim(cells, cells.shape[dim] - width, cells.shape[dim], axis=dim)
        cells = jnp.concatenate(
            [
                lax.ppermute(tail, axis, [(i, (i + 1) % count) for i in range(ends)]),
                cells,
                lax.ppermute(head, axis, [((i + 1) % count, i) for i in range(ends)]),
            ],
            axis=dim,
        )
    return cells


def gather_rows(cells, axis):
    count = lax.axis_size(axis)
    me = lax.axis_index(axis)
    parts = [cells] + [
        lax.ppermute(cells, axis, [(i, (i + s) % count) for i in range(count)])
        for s in range(1, count)
    ]
    stacked = jnp.stack(parts)
    return jnp.take(stacked, (me - jnp.arange(count)) % count, axis=0)


def split3(value):
    parts = []
    rest = value
    for _ in range(3):
        part = lax.reduce_precision(rest, exponent_bits=8, mantissa_bits=7)
        parts.append(part.astype(jnp.bfloat16))
        rest = rest - part
    return jnp.stack(parts)


def join3(parts):
    return (parts[0].astype(jnp.float32) + parts[1].astype(jnp.float32)) + parts[2].astype(jnp.float32)


def silu_act(value):
    return value * jax.nn.sigmoid(value)


def shards(
    video,
    cache,
    conv_weight,
    conv_bias,
    down_weight,
    patch_weight,
    step_index,
    mod_weight,
    qkv_weight,
):
    cin = conv_weight.shape[2] // 3
    cmid = conv_weight.shape[3]
    frame_count = video.shape[0]
    tile_rows = video.shape[1]
    tile_cols = video.shape[2] // cin
    n_ctx = lax.axis_size("ctx")
    c_idx = lax.axis_index("ctx")
    heads_here = qkv_weight.shape[1]
    out_cols = heads_here * 3 * HDIM
    local = qkv_weight.reshape(qkv_weight.shape[0], out_cols)
    rows = local.shape[0]
    half_rows = rows // 2
    quarter_rows = half_rows // 2
    core = lax.axis_index("dp") % 2
    mine = lax.dynamic_slice_in_dim(local, core * half_rows, half_rows, 0)
    n_dp = lax.axis_size("dp")

    def send(cells, step):
        return lax.ppermute(cells, "ctx", [(i, step(i)) for i in range(n_ctx)])

    def swap(cells):
        return lax.ppermute(cells, "dp", [(i, i ^ 1) for i in range(n_dp)])

    up = lambda i: (i + 2) % n_ctx
    down = lambda i: (i + n_ctx - 2) % n_ctx
    across = lambda i: i ^ 1
    from_up = (c_idx + n_ctx - 2) % n_ctx
    from_down = (c_idx + 2) % n_ctx
    opposite = (c_idx + 4) % n_ctx
    a_up = send(mine, up)
    a_down = send(mine, down)
    a_across = send(mine, across)
    b_up = send(a_up[:quarter_rows], up)
    b_down = send(a_down[quarter_rows:], down)
    b_across_up = send(a_across, up)
    b_across_down = send(a_across, down)
    c_first = send(b_up, across)
    c_second = send(b_down, across)
    stages = [
        [(a_up, from_up, 0), (a_down, from_down, 0), (a_across, c_idx ^ 1, 0)],
        [(b_up, opposite, 0), (b_down, opposite, quarter_rows),
         (b_across_up, from_up ^ 1, 0), (b_across_down, from_down ^ 1, 0)],
        [(c_first, opposite ^ 1, 0), (c_second, opposite ^ 1, quarter_rows)],
    ]
    stages = [
        (stage, ours, swap(ours))
        for stage, ours in ((s, jnp.concatenate([cells for cells, _, _ in s], 0)) for s in stages)
    ]
    frames = jnp.concatenate([cache, video], 0).reshape(frame_count + 2, tile_rows, tile_cols, cin)
    padded = with_halo(frames, (("head", 1), ("ctx", 2)), 1)
    total = jnp.zeros((frame_count, tile_rows, tile_cols, cmid), jnp.float32)
    for time_tap in range(3):
        for row_tap in range(3):
            slab = padded[time_tap : time_tap + frame_count, row_tap : row_tap + tile_rows]
            stacked = jnp.concatenate(
                [slab[:, :, col_tap : col_tap + tile_cols] for col_tap in range(3)], -1
            )
            total = total + jnp.einsum(
                "fyxc,cd->fyxd",
                stacked,
                conv_weight[time_tap, row_tap],
                preferred_element_type=jnp.float32,
            )
    hidden = silu_act(total + conv_bias).astype(jnp.bfloat16)
    stacked = (
        hidden.reshape(frame_count, tile_rows // 2, 2, tile_cols // 2, 2, cmid)
        .transpose(0, 1, 3, 2, 4, 5)
        .reshape(-1, 4 * cmid)
    )
    reduced = silu_act(jnp.dot(stacked, down_weight, preferred_element_type=jnp.float32)).astype(
        jnp.bfloat16
    )
    reduced = reduced.reshape(frame_count, tile_rows // 2, tile_cols // 2, cmid)
    patches = reduced.reshape(frame_count, tile_rows // 4, 2, tile_cols // 4, 2, cmid).transpose(
        0, 1, 3, 2, 4, 5
    )
    patches = patches.reshape(-1, 4 * cmid)
    half = FREQ // 2
    freqs = jnp.exp(-jnp.log(10000.0) * jnp.arange(half, dtype=jnp.float32) / half)
    angles = step_index[0].astype(jnp.float32) * freqs
    timing = jnp.concatenate([jnp.cos(angles), jnp.sin(angles)]).astype(jnp.bfloat16)
    mod_share = jnp.dot(timing[None, :], mod_weight, preferred_element_type=jnp.float32)[0]
    n_head = lax.axis_size("head")
    n_ctx = lax.axis_size("ctx")
    h_idx = lax.axis_index("head")
    c_idx = lax.axis_index("ctx")
    quarter = D // n_head
    share_width = patch_weight.shape[1]
    share_parts = split3(mod_share).reshape(-1, share_width)
    carried = lax.all_gather(
        jnp.concatenate([patch_weight, share_parts], 0), "ctx", axis=1, tiled=True
    )
    weight_quarter = carried[: patch_weight.shape[0]]
    row_share = (
        carried[patch_weight.shape[0] :]
        .reshape(-1, n_ctx, share_width)
        .transpose(1, 0, 2)
        .reshape(n_ctx, 3, -1)
        .transpose(1, 0, 2)
        .reshape(3, -1)
    )
    row_parts = join3(row_share)
    block_patches = gather_rows(patches, "head").reshape(-1, patches.shape[1])
    embedded = jnp.dot(block_patches, weight_quarter, preferred_element_type=jnp.float32)
    token_count = embedded.shape[0]
    riding = gather_rows(jnp.concatenate([jnp.sum(embedded * embedded, -1), row_parts]), "head")
    squares = riding[:, :token_count]
    modulation = riding[:, token_count:].reshape(-1)
    scale = lax.dynamic_slice_in_dim(modulation, h_idx * quarter, quarter)
    shift = lax.dynamic_slice_in_dim(modulation, D + h_idx * quarter, quarter)
    inverse = lax.rsqrt(jnp.sum(squares, 0) / D + 1e-06)[:, None]
    normed_quarter = (embedded * inverse * (1.0 + scale) + shift).astype(jnp.bfloat16)
    normed = lax.all_gather(normed_quarter, "head", axis=1, tiled=True)
    group_rows = normed.shape[0]
    heads_here = qkv_weight.shape[1]
    out_cols = heads_here * 3 * HDIM
    qkv = None
    for number, (stage, ours, theirs) in enumerate(stages):
        weights = [local] if number == 0 else []
        columns = [lax.dynamic_slice_in_dim(normed, c_idx * rows, rows, 1)] if number == 0 else []
        weights += [ours, theirs]
        for side in (core, 1 - core):
            for cells, block, offset in stage:
                columns.append(
                    lax.dynamic_slice_in_dim(
                        normed, block * rows + side * half_rows + offset, cells.shape[0], 1
                    )
                )
        part = jnp.dot(
            jnp.concatenate(columns, 1),
            jnp.concatenate(weights, 0),
            preferred_element_type=jnp.float32,
        )
        qkv = part if qkv is None else qkv + part
    qkv = qkv.astype(jnp.bfloat16).reshape(group_rows, heads_here, 3, HDIM)
    active = min(heads_here, n_ctx)
    spare = n_ctx - active
    outgoing = jnp.concatenate(
        [qkv.transpose(1, 0, 2, 3), jnp.zeros((spare,) + qkv.shape[:1] + qkv.shape[2:], qkv.dtype)], 0
    )
    triple = lax.all_to_all(outgoing, "ctx", 0, 0, tiled=True)
    keys = triple[:, :, 1].reshape(-1, HDIM)
    values = triple[:, :, 2].reshape(-1, HDIM)
    inv_root = 1.0 / jnp.sqrt(jnp.float32(HDIM))

    def one_block(query):
        scores = jnp.dot(query, keys.T, preferred_element_type=jnp.float32) * inv_root
        best = jnp.maximum(jnp.float32(-1e30), jnp.max(scores, -1))
        probs = jnp.exp(scores - best[:, None])
        denom = jnp.sum(probs, -1)
        accum = jnp.dot(probs.astype(jnp.bfloat16), values, preferred_element_type=jnp.float32)
        return (accum / denom[:, None]).astype(jnp.bfloat16)

    attended = lax.map(one_block, triple[:, :, 0])
    by_head = lax.all_to_all(attended, "ctx", 0, 0, tiled=True)[:heads_here]
    return by_head.transpose(1, 0, 2).reshape(group_rows, heads_here * HDIM)


def solution(mesh):
    return jax.shard_map(
        shards,
        mesh=mesh,
        in_specs=(
            P("dp", "head", "ctx"),
            P("dp", "head", "ctx"),
            P(),
            P(),
            P(),
            P(None, ("head", "ctx")),
            P("dp"),
            P(None, ("head", "ctx")),
            P("ctx", "head", None, None),
        ),
        out_specs=P(("dp", "ctx"), "head"),
        check_vma=False,
    )
```

```python
import jax
import jax.numpy as jnp
from jax import lax
from jax.sharding import PartitionSpec as P

D = 5120
HDIM = 128
FREQ = 256


def with_halo(cells, sides, width):
    for axis, dim in sides:
        count = lax.axis_size(axis)
        ends = count - 1
        head = lax.slice_in_dim(cells, 0, width, axis=dim)
        tail = lax.slice_in_dim(cells, cells.shape[dim] - width, cells.shape[dim], axis=dim)
        cells = jnp.concatenate(
            [
                lax.ppermute(tail, axis, [(i, (i + 1) % count) for i in range(ends)]),
                cells,
                lax.ppermute(head, axis, [((i + 1) % count, i) for i in range(ends)]),
            ],
            axis=dim,
        )
    return cells


def gather_rows(cells, axis):
    count = lax.axis_size(axis)
    me = lax.axis_index(axis)
    parts = [cells] + [
        lax.ppermute(cells, axis, [(i, (i + s) % count) for i in range(count)])
        for s in range(1, count)
    ]
    stacked = jnp.stack(parts)
    return jnp.take(stacked, (me - jnp.arange(count)) % count, axis=0)


def split3(value):
    parts = []
    rest = value
    for _ in range(3):
        part = lax.reduce_precision(rest, exponent_bits=8, mantissa_bits=7)
        parts.append(part.astype(jnp.bfloat16))
        rest = rest - part
    return jnp.stack(parts)


def join3(parts):
    return (parts[0].astype(jnp.float32) + parts[1].astype(jnp.float32)) + parts[2].astype(jnp.float32)


def silu_act(value):
    return value * jax.nn.sigmoid(value)


def shards(
    video,
    cache,
    conv_weight,
    conv_bias,
    down_weight,
    patch_weight,
    step_index,
    mod_weight,
    qkv_weight,
):
    cin = conv_weight.shape[2] // 3
    cmid = conv_weight.shape[3]
    frame_count = video.shape[0]
    tile_rows = video.shape[1]
    tile_cols = video.shape[2] // cin
    n_ctx = lax.axis_size("ctx")
    c_idx = lax.axis_index("ctx")
    heads_here = qkv_weight.shape[1]
    out_cols = heads_here * 3 * HDIM
    local = qkv_weight.reshape(qkv_weight.shape[0], out_cols)
    rows = local.shape[0]
    half_rows = rows // 2
    quarter_rows = half_rows // 2
    core = lax.axis_index("dp") % 2
    mine = lax.dynamic_slice_in_dim(local, core * half_rows, half_rows, 0)
    n_dp = lax.axis_size("dp")

    def send(cells, step):
        return lax.ppermute(cells, "ctx", [(i, step(i)) for i in range(n_ctx)])

    def swap(cells):
        return lax.ppermute(cells, "dp", [(i, i ^ 1) for i in range(n_dp)])

    up = lambda i: (i + 2) % n_ctx
    down = lambda i: (i + n_ctx - 2) % n_ctx
    across = lambda i: i ^ 1
    from_up = (c_idx + n_ctx - 2) % n_ctx
    from_down = (c_idx + 2) % n_ctx
    opposite = (c_idx + 4) % n_ctx
    a_up = send(mine, up)
    a_down = send(mine, down)
    a_across = send(mine, across)
    b_up = send(a_up[:quarter_rows], up)
    b_down = send(a_down[quarter_rows:], down)
    b_across_up = send(a_across, up)
    b_across_down = send(a_across, down)
    c_first = send(b_up, across)
    c_second = send(b_down, across)
    stages = [
        [(a_up, from_up, 0), (a_down, from_down, 0), (a_across, c_idx ^ 1, 0)],
        [(b_up, opposite, 0), (b_down, opposite, quarter_rows),
         (b_across_up, from_up ^ 1, 0), (b_across_down, from_down ^ 1, 0)],
        [(c_first, opposite ^ 1, 0), (c_second, opposite ^ 1, quarter_rows)],
    ]
    stages = [
        (stage, ours, swap(ours))
        for stage, ours in ((s, jnp.concatenate([cells for cells, _, _ in s], 0)) for s in stages)
    ]
    frames = jnp.concatenate([cache, video], 0).reshape(frame_count + 2, tile_rows, tile_cols, cin)
    padded = with_halo(frames, (("head", 1), ("ctx", 2)), 1)
    total = jnp.zeros((frame_count, tile_rows, tile_cols, cmid), jnp.float32)
    for time_tap in range(3):
        for row_tap in range(3):
            slab = padded[time_tap : time_tap + frame_count, row_tap : row_tap + tile_rows]
            stacked = jnp.concatenate(
                [slab[:, :, col_tap : col_tap + tile_cols] for col_tap in range(3)], -1
            )
            total = total + jnp.einsum(
                "fyxc,cd->fyxd",
                stacked,
                conv_weight[time_tap, row_tap],
                preferred_element_type=jnp.float32,
            )
    hidden = silu_act(total + conv_bias).astype(jnp.bfloat16)
    stacked = (
        hidden.reshape(frame_count, tile_rows // 2, 2, tile_cols // 2, 2, cmid)
        .transpose(0, 1, 3, 2, 4, 5)
        .reshape(-1, 4 * cmid)
    )
    reduced = silu_act(jnp.dot(stacked, down_weight, preferred_element_type=jnp.float32)).astype(
        jnp.bfloat16
    )
    reduced = reduced.reshape(frame_count, tile_rows // 2, tile_cols // 2, cmid)
    patches = reduced.reshape(frame_count, tile_rows // 4, 2, tile_cols // 4, 2, cmid).transpose(
        0, 1, 3, 2, 4, 5
    )
    patches = patches.reshape(-1, 4 * cmid)
    half = FREQ // 2
    freqs = jnp.exp(-jnp.log(10000.0) * jnp.arange(half, dtype=jnp.float32) / half)
    angles = step_index[0].astype(jnp.float32) * freqs
    timing = jnp.concatenate([jnp.cos(angles), jnp.sin(angles)]).astype(jnp.bfloat16)
    mod_share = jnp.dot(timing[None, :], mod_weight, preferred_element_type=jnp.float32)[0]
    n_head = lax.axis_size("head")
    n_ctx = lax.axis_size("ctx")
    h_idx = lax.axis_index("head")
    c_idx = lax.axis_index("ctx")
    quarter = D // n_head
    share_width = patch_weight.shape[1]
    share_parts = split3(mod_share).reshape(-1, share_width)
    carried = lax.all_gather(
        jnp.concatenate([patch_weight, share_parts], 0), "ctx", axis=1, tiled=True
    )
    weight_quarter = carried[: patch_weight.shape[0]]
    row_share = (
        carried[patch_weight.shape[0] :]
        .reshape(-1, n_ctx, share_width)
        .transpose(1, 0, 2)
        .reshape(n_ctx, 3, -1)
        .transpose(1, 0, 2)
        .reshape(3, -1)
    )
    row_parts = join3(row_share)
    block_patches = gather_rows(patches, "head").reshape(-1, patches.shape[1])
    embedded = jnp.dot(block_patches, weight_quarter, preferred_element_type=jnp.float32)
    token_count = embedded.shape[0]
    riding = gather_rows(jnp.concatenate([jnp.sum(embedded * embedded, -1), row_parts]), "head")
    squares = riding[:, :token_count]
    modulation = riding[:, token_count:].reshape(-1)
    scale = lax.dynamic_slice_in_dim(modulation, h_idx * quarter, quarter)
    shift = lax.dynamic_slice_in_dim(modulation, D + h_idx * quarter, quarter)
    inverse = lax.rsqrt(jnp.sum(squares, 0) / D + 1e-06)[:, None]
    normed_quarter = (embedded * inverse * (1.0 + scale) + shift).astype(jnp.bfloat16)
    normed = lax.all_gather(normed_quarter, "head", axis=1, tiled=True)
    group_rows = normed.shape[0]
    heads_here = qkv_weight.shape[1]
    out_cols = heads_here * 3 * HDIM
    qkv = None
    for number, (stage, ours, theirs) in enumerate(stages):
        weights = [local] if number == 0 else []
        columns = [lax.dynamic_slice_in_dim(normed, c_idx * rows, rows, 1)] if number == 0 else []
        weights += [ours, theirs]
        for side in (core, 1 - core):
            for cells, block, offset in stage:
                columns.append(
                    lax.dynamic_slice_in_dim(
                        normed, block * rows + side * half_rows + offset, cells.shape[0], 1
                    )
                )
        part = jnp.dot(
            jnp.concatenate(columns, 1),
            jnp.concatenate(weights, 0),
            preferred_element_type=jnp.float32,
        )
        qkv = part if qkv is None else qkv + part
    qkv = qkv.astype(jnp.bfloat16).reshape(group_rows, heads_here, 3, HDIM)
    active = min(heads_here, n_ctx)
    spare = n_ctx - active
    by_part = qkv.transpose(1, 2, 0, 3)
    outgoing = jnp.concatenate([by_part, jnp.zeros((spare,) + by_part.shape[1:], qkv.dtype)], 0)
    triple = lax.all_to_all(outgoing, "ctx", 0, 0, tiled=True)
    keys = triple[:, 1].reshape(-1, HDIM)
    values = triple[:, 2].reshape(-1, HDIM)
    inv_root = 1.0 / jnp.sqrt(jnp.float32(HDIM))

    def one_block(query):
        scores = jnp.dot(query, keys.T, preferred_element_type=jnp.float32) * inv_root
        best = jnp.maximum(jnp.float32(-1e30), jnp.max(scores, -1))
        probs = jnp.exp(scores - best[:, None])
        denom = jnp.sum(probs, -1)
        accum = jnp.dot(probs.astype(jnp.bfloat16), values, preferred_element_type=jnp.float32)
        return (accum / denom[:, None]).astype(jnp.bfloat16)

    attended = lax.map(one_block, triple[:, 0])
    by_head = lax.all_to_all(attended, "ctx", 0, 0, tiled=True)[:heads_here]
    return by_head.transpose(1, 0, 2).reshape(group_rows, heads_here * HDIM)


def solution(mesh):
    return jax.shard_map(
        shards,
        mesh=mesh,
        in_specs=(
            P("dp", "head", "ctx"),
            P("dp", "head", "ctx"),
            P(),
            P(),
            P(),
            P(None, ("head", "ctx")),
            P("dp"),
            P(None, ("head", "ctx")),
            P("ctx", "head", None, None),
        ),
        out_specs=P(("dp", "ctx"), "head"),
        check_vma=False,
    )
```

```python
import jax
import jax.numpy as jnp
from jax import lax
from jax.sharding import PartitionSpec as P

D = 5120
HDIM = 128
FREQ = 256


def with_halo(cells, sides, width):
    for axis, dim in sides:
        count = lax.axis_size(axis)
        ends = count - 1
        head = lax.slice_in_dim(cells, 0, width, axis=dim)
        tail = lax.slice_in_dim(cells, cells.shape[dim] - width, cells.shape[dim], axis=dim)
        cells = jnp.concatenate(
            [
                lax.ppermute(tail, axis, [(i, (i + 1) % count) for i in range(ends)]),
                cells,
                lax.ppermute(head, axis, [((i + 1) % count, i) for i in range(ends)]),
            ],
            axis=dim,
        )
    return cells


def gather_rows(cells, axis):
    count = lax.axis_size(axis)
    me = lax.axis_index(axis)
    parts = [cells] + [
        lax.ppermute(cells, axis, [(i, (i + s) % count) for i in range(count)])
        for s in range(1, count)
    ]
    stacked = jnp.stack(parts)
    return jnp.take(stacked, (me - jnp.arange(count)) % count, axis=0)


def split3(value):
    parts = []
    rest = value
    for _ in range(3):
        part = lax.reduce_precision(rest, exponent_bits=8, mantissa_bits=7)
        parts.append(part.astype(jnp.bfloat16))
        rest = rest - part
    return jnp.stack(parts)


def join3(parts):
    return (parts[0].astype(jnp.float32) + parts[1].astype(jnp.float32)) + parts[2].astype(jnp.float32)


def silu_act(value):
    return value * jax.nn.sigmoid(value)


def shards(
    video,
    cache,
    conv_weight,
    conv_bias,
    down_weight,
    patch_weight,
    step_index,
    mod_weight,
    qkv_weight,
):
    cin = conv_weight.shape[2] // 3
    cmid = conv_weight.shape[3]
    frame_count = video.shape[0]
    tile_rows = video.shape[1]
    tile_cols = video.shape[2] // cin
    n_ctx = lax.axis_size("ctx")
    c_idx = lax.axis_index("ctx")
    heads_here = qkv_weight.shape[1]
    out_cols = heads_here * 3 * HDIM
    local = qkv_weight.reshape(qkv_weight.shape[0], out_cols)
    rows = local.shape[0]
    half_rows = rows // 2
    quarter_rows = half_rows // 2
    core = lax.axis_index("dp") % 2
    mine = lax.dynamic_slice_in_dim(local, core * half_rows, half_rows, 0)
    n_dp = lax.axis_size("dp")

    def send(cells, step):
        return lax.ppermute(cells, "ctx", [(i, step(i)) for i in range(n_ctx)])

    def swap(cells):
        return lax.ppermute(cells, "dp", [(i, i ^ 1) for i in range(n_dp)])

    up = lambda i: (i + 2) % n_ctx
    down = lambda i: (i + n_ctx - 2) % n_ctx
    across = lambda i: i ^ 1
    from_up = (c_idx + n_ctx - 2) % n_ctx
    from_down = (c_idx + 2) % n_ctx
    opposite = (c_idx + 4) % n_ctx
    a_up = send(mine, up)
    a_down = send(mine, down)
    a_across = send(mine, across)
    b_up = send(a_up[:quarter_rows], up)
    b_down = send(a_down[quarter_rows:], down)
    b_across_up = send(a_across, up)
    b_across_down = send(a_across, down)
    c_first = send(b_up, across)
    c_second = send(b_down, across)
    stages = [
        [(a_up, from_up, 0), (a_down, from_down, 0), (a_across, c_idx ^ 1, 0)],
        [(b_up, opposite, 0), (b_down, opposite, quarter_rows),
         (b_across_up, from_up ^ 1, 0), (b_across_down, from_down ^ 1, 0)],
        [(c_first, opposite ^ 1, 0), (c_second, opposite ^ 1, quarter_rows)],
    ]
    stages = [
        (stage, ours, swap(ours))
        for stage, ours in ((s, jnp.concatenate([cells for cells, _, _ in s], 0)) for s in stages)
    ]
    frames = jnp.concatenate([cache, video], 0).reshape(frame_count + 2, tile_rows, tile_cols, cin)
    padded = with_halo(frames, (("head", 1), ("ctx", 2)), 1)
    total = jnp.zeros((frame_count, tile_rows, tile_cols, cmid), jnp.float32)
    for time_tap in range(3):
        for row_tap in range(3):
            slab = padded[time_tap : time_tap + frame_count, row_tap : row_tap + tile_rows]
            stacked = jnp.concatenate(
                [slab[:, :, col_tap : col_tap + tile_cols] for col_tap in range(3)], -1
            )
            total = total + jnp.einsum(
                "fyxc,cd->fyxd",
                stacked,
                conv_weight[time_tap, row_tap],
                preferred_element_type=jnp.float32,
            )
    hidden = silu_act(total + conv_bias).astype(jnp.bfloat16)
    stacked = (
        hidden.reshape(frame_count, tile_rows // 2, 2, tile_cols // 2, 2, cmid)
        .transpose(0, 1, 3, 2, 4, 5)
        .reshape(-1, 4 * cmid)
    )
    reduced = silu_act(jnp.dot(stacked, down_weight, preferred_element_type=jnp.float32)).astype(
        jnp.bfloat16
    )
    reduced = reduced.reshape(frame_count, tile_rows // 2, tile_cols // 2, cmid)
    patches = reduced.reshape(frame_count, tile_rows // 4, 2, tile_cols // 4, 2, cmid).transpose(
        0, 1, 3, 2, 4, 5
    )
    patches = patches.reshape(-1, 4 * cmid)
    half = FREQ // 2
    freqs = jnp.exp(-jnp.log(10000.0) * jnp.arange(half, dtype=jnp.float32) / half)
    angles = step_index[0].astype(jnp.float32) * freqs
    timing = jnp.concatenate([jnp.cos(angles), jnp.sin(angles)]).astype(jnp.bfloat16)
    mod_share = jnp.dot(timing[None, :], mod_weight, preferred_element_type=jnp.float32)[0]
    n_head = lax.axis_size("head")
    n_ctx = lax.axis_size("ctx")
    h_idx = lax.axis_index("head")
    c_idx = lax.axis_index("ctx")
    quarter = D // n_head
    share_width = patch_weight.shape[1]
    share_parts = split3(mod_share).reshape(-1, share_width)
    carried = lax.all_gather(
        jnp.concatenate([patch_weight, share_parts], 0), "ctx", axis=1, tiled=True
    )
    weight_quarter = carried[: patch_weight.shape[0]]
    row_share = (
        carried[patch_weight.shape[0] :]
        .reshape(-1, n_ctx, share_width)
        .transpose(1, 0, 2)
        .reshape(n_ctx, 3, -1)
        .transpose(1, 0, 2)
        .reshape(3, -1)
    )
    row_parts = join3(row_share)
    block_patches = gather_rows(patches, "head").reshape(-1, patches.shape[1])
    embedded = jnp.dot(block_patches, weight_quarter, preferred_element_type=jnp.float32)
    token_count = embedded.shape[0]
    riding = gather_rows(jnp.concatenate([jnp.sum(embedded * embedded, -1), row_parts]), "head")
    squares = riding[:, :token_count]
    modulation = riding[:, token_count:].reshape(-1)
    scale = lax.dynamic_slice_in_dim(modulation, h_idx * quarter, quarter)
    shift = lax.dynamic_slice_in_dim(modulation, D + h_idx * quarter, quarter)
    inverse = lax.rsqrt(jnp.sum(squares, 0) / D + 1e-06)[:, None]
    normed_quarter = (embedded * inverse * (1.0 + scale) + shift).astype(jnp.bfloat16)
    normed = lax.all_gather(normed_quarter, "head", axis=1, tiled=True)
    group_rows = normed.shape[0]
    heads_here = qkv_weight.shape[1]
    out_cols = heads_here * 3 * HDIM
    qkv = None
    for number, (stage, ours, theirs) in enumerate(stages):
        weights = [local] if number == 0 else []
        columns = [lax.dynamic_slice_in_dim(normed, c_idx * rows, rows, 1)] if number == 0 else []
        weights += [ours, theirs]
        for side in (core, 1 - core):
            for cells, block, offset in stage:
                columns.append(
                    lax.dynamic_slice_in_dim(
                        normed, block * rows + side * half_rows + offset, cells.shape[0], 1
                    )
                )
        part = jnp.dot(
            jnp.concatenate(columns, 1),
            jnp.concatenate(weights, 0),
            preferred_element_type=jnp.float32,
        )
        qkv = part if qkv is None else qkv + part
    qkv = qkv.astype(jnp.bfloat16).reshape(group_rows, heads_here, 3, HDIM)
    active = min(heads_here, n_ctx)
    spare = n_ctx - active
    by_part = qkv.transpose(1, 2, 0, 3)
    outgoing = jnp.concatenate([by_part, jnp.zeros((spare,) + by_part.shape[1:], qkv.dtype)], 0)
    triple = lax.all_to_all(outgoing, "ctx", 0, 0, tiled=True)
    keys = triple[:, 1].reshape(-1, HDIM)
    values = triple[:, 2].reshape(-1, HDIM)
    inv_root = 1.0 / jnp.sqrt(jnp.float32(HDIM))

    def one_block(query):
        scores = jnp.dot(query, keys.T, preferred_element_type=jnp.float32) * inv_root
        best = jnp.maximum(jnp.float32(-1e30), jnp.max(scores, -1))
        probs = jnp.exp(scores - best[:, None])
        denom = jnp.sum(probs, -1)
        accum = jnp.dot(probs.astype(jnp.bfloat16), values, preferred_element_type=jnp.float32)
        return (accum / denom[:, None]).astype(jnp.bfloat16)

    queries = triple[:, 0]
    chunks = 4
    attended = lax.map(one_block, queries.reshape(chunks, -1, HDIM)).reshape(queries.shape)
    by_head = lax.all_to_all(attended, "ctx", 0, 0, tiled=True)[:heads_here]
    return by_head.transpose(1, 0, 2).reshape(group_rows, heads_here * HDIM)


def solution(mesh):
    return jax.shard_map(
        shards,
        mesh=mesh,
        in_specs=(
            P("dp", "head", "ctx"),
            P("dp", "head", "ctx"),
            P(),
            P(),
            P(),
            P(None, ("head", "ctx")),
            P("dp"),
            P(None, ("head", "ctx")),
            P("ctx", "head", None, None),
        ),
        out_specs=P(("dp", "ctx"), "head"),
        check_vma=False,
    )
```

```python
import jax
import jax.numpy as jnp
from jax import lax
from jax.sharding import PartitionSpec as P

D = 5120
HDIM = 128
FREQ = 256


def with_halo(cells, sides, width):
    for axis, dim in sides:
        count = lax.axis_size(axis)
        ends = count - 1
        head = lax.slice_in_dim(cells, 0, width, axis=dim)
        tail = lax.slice_in_dim(cells, cells.shape[dim] - width, cells.shape[dim], axis=dim)
        cells = jnp.concatenate(
            [
                lax.ppermute(tail, axis, [(i, (i + 1) % count) for i in range(ends)]),
                cells,
                lax.ppermute(head, axis, [((i + 1) % count, i) for i in range(ends)]),
            ],
            axis=dim,
        )
    return cells


def gather_rows(cells, axis):
    count = lax.axis_size(axis)
    me = lax.axis_index(axis)
    parts = [cells] + [
        lax.ppermute(cells, axis, [(i, (i + s) % count) for i in range(count)])
        for s in range(1, count)
    ]
    stacked = jnp.stack(parts)
    return jnp.take(stacked, (me - jnp.arange(count)) % count, axis=0)


def split3(value):
    parts = []
    rest = value
    for _ in range(3):
        part = lax.reduce_precision(rest, exponent_bits=8, mantissa_bits=7)
        parts.append(part.astype(jnp.bfloat16))
        rest = rest - part
    return jnp.stack(parts)


def join3(parts):
    return (parts[0].astype(jnp.float32) + parts[1].astype(jnp.float32)) + parts[2].astype(jnp.float32)


def silu_act(value):
    return value * jax.nn.sigmoid(value)


def shards(
    video,
    cache,
    conv_weight,
    conv_bias,
    down_weight,
    patch_weight,
    step_index,
    mod_weight,
    qkv_weight,
):
    cin = conv_weight.shape[2] // 3
    cmid = conv_weight.shape[3]
    frame_count = video.shape[0]
    tile_rows = video.shape[1]
    tile_cols = video.shape[2] // cin
    n_ctx = lax.axis_size("ctx")
    c_idx = lax.axis_index("ctx")
    heads_here = qkv_weight.shape[1]
    out_cols = heads_here * 3 * HDIM
    local = qkv_weight.reshape(qkv_weight.shape[0], out_cols)
    rows = local.shape[0]
    half_rows = rows // 2
    quarter_rows = half_rows // 2
    core = lax.axis_index("dp") % 2
    mine = lax.dynamic_slice_in_dim(local, core * half_rows, half_rows, 0)
    n_dp = lax.axis_size("dp")

    def send(cells, step):
        return lax.ppermute(cells, "ctx", [(i, step(i)) for i in range(n_ctx)])

    def swap(cells):
        return lax.ppermute(cells, "dp", [(i, i ^ 1) for i in range(n_dp)])

    up = lambda i: (i + 2) % n_ctx
    down = lambda i: (i + n_ctx - 2) % n_ctx
    across = lambda i: i ^ 1
    from_up = (c_idx + n_ctx - 2) % n_ctx
    from_down = (c_idx + 2) % n_ctx
    opposite = (c_idx + 4) % n_ctx
    a_up = send(mine, up)
    a_down = send(mine, down)
    a_across = send(mine, across)
    b_up = send(a_up[:quarter_rows], up)
    b_down = send(a_down[quarter_rows:], down)
    b_across_up = send(a_across, up)
    b_across_down = send(a_across, down)
    c_first = send(b_up, across)
    c_second = send(b_down, across)
    stages = [
        [(a_up, from_up, 0), (a_down, from_down, 0), (a_across, c_idx ^ 1, 0)],
        [(b_up, opposite, 0), (b_down, opposite, quarter_rows),
         (b_across_up, from_up ^ 1, 0), (b_across_down, from_down ^ 1, 0)],
        [(c_first, opposite ^ 1, 0), (c_second, opposite ^ 1, quarter_rows)],
    ]
    stages = [
        (stage, ours, swap(ours))
        for stage, ours in ((s, jnp.concatenate([cells for cells, _, _ in s], 0)) for s in stages)
    ]
    frames = jnp.concatenate([cache, video], 0).reshape(frame_count + 2, tile_rows, tile_cols, cin)
    padded = with_halo(frames, (("head", 1), ("ctx", 2)), 1)
    total = jnp.zeros((frame_count, tile_rows, tile_cols, cmid), jnp.float32)
    for time_tap in range(3):
        for row_tap in range(3):
            slab = padded[time_tap : time_tap + frame_count, row_tap : row_tap + tile_rows]
            stacked = jnp.concatenate(
                [slab[:, :, col_tap : col_tap + tile_cols] for col_tap in range(3)], -1
            )
            total = total + jnp.einsum(
                "fyxc,cd->fyxd",
                stacked,
                conv_weight[time_tap, row_tap],
                preferred_element_type=jnp.float32,
            )
    hidden = silu_act(total + conv_bias).astype(jnp.bfloat16)
    stacked = (
        hidden.reshape(frame_count, tile_rows // 2, 2, tile_cols // 2, 2, cmid)
        .transpose(0, 1, 3, 2, 4, 5)
        .reshape(-1, 4 * cmid)
    )
    reduced = silu_act(jnp.dot(stacked, down_weight, preferred_element_type=jnp.float32)).astype(
        jnp.bfloat16
    )
    reduced = reduced.reshape(frame_count, tile_rows // 2, tile_cols // 2, cmid)
    patches = reduced.reshape(frame_count, tile_rows // 4, 2, tile_cols // 4, 2, cmid).transpose(
        0, 1, 3, 2, 4, 5
    )
    patches = patches.reshape(-1, 4 * cmid)
    half = FREQ // 2
    freqs = jnp.exp(-jnp.log(10000.0) * jnp.arange(half, dtype=jnp.float32) / half)
    angles = step_index[0].astype(jnp.float32) * freqs
    timing = jnp.concatenate([jnp.cos(angles), jnp.sin(angles)]).astype(jnp.bfloat16)
    mod_share = jnp.dot(timing[None, :], mod_weight, preferred_element_type=jnp.float32)[0]
    n_head = lax.axis_size("head")
    n_ctx = lax.axis_size("ctx")
    h_idx = lax.axis_index("head")
    c_idx = lax.axis_index("ctx")
    quarter = D // n_head
    share_width = patch_weight.shape[1]
    share_parts = split3(mod_share).reshape(-1, share_width)
    carried = lax.all_gather(
        jnp.concatenate([patch_weight, share_parts], 0), "ctx", axis=1, tiled=True
    )
    weight_quarter = carried[: patch_weight.shape[0]]
    row_share = (
        carried[patch_weight.shape[0] :]
        .reshape(-1, n_ctx, share_width)
        .transpose(1, 0, 2)
        .reshape(n_ctx, 3, -1)
        .transpose(1, 0, 2)
        .reshape(3, -1)
    )
    row_parts = join3(row_share)
    block_patches = gather_rows(patches, "head").reshape(-1, patches.shape[1])
    embedded = jnp.dot(block_patches, weight_quarter, preferred_element_type=jnp.float32)
    token_count = embedded.shape[0]
    riding = gather_rows(jnp.concatenate([jnp.sum(embedded * embedded, -1), row_parts]), "head")
    squares = riding[:, :token_count]
    modulation = riding[:, token_count:].reshape(-1)
    scale = lax.dynamic_slice_in_dim(modulation, h_idx * quarter, quarter)
    shift = lax.dynamic_slice_in_dim(modulation, D + h_idx * quarter, quarter)
    inverse = lax.rsqrt(jnp.sum(squares, 0) / D + 1e-06)[:, None]
    normed_quarter = (embedded * inverse * (1.0 + scale) + shift).astype(jnp.bfloat16)
    normed = lax.all_gather(normed_quarter, "head", axis=1, tiled=True)
    group_rows = normed.shape[0]
    heads_here = qkv_weight.shape[1]
    out_cols = heads_here * 3 * HDIM
    qkv = None
    for number, (stage, ours, theirs) in enumerate(stages):
        weights = [local] if number == 0 else []
        columns = [lax.dynamic_slice_in_dim(normed, c_idx * rows, rows, 1)] if number == 0 else []
        weights += [ours, theirs]
        for side in (core, 1 - core):
            for cells, block, offset in stage:
                columns.append(
                    lax.dynamic_slice_in_dim(
                        normed, block * rows + side * half_rows + offset, cells.shape[0], 1
                    )
                )
        part = jnp.dot(
            jnp.concatenate(columns, 1),
            jnp.concatenate(weights, 0),
            preferred_element_type=jnp.float32,
        )
        qkv = part if qkv is None else qkv + part
    qkv = qkv.astype(jnp.bfloat16).reshape(group_rows, heads_here, 3, HDIM)
    active = min(heads_here, n_ctx)
    spare = n_ctx - active
    by_part = qkv.transpose(1, 2, 0, 3)
    outgoing = jnp.concatenate([by_part, jnp.zeros((spare,) + by_part.shape[1:], qkv.dtype)], 0)
    triple = lax.all_to_all(outgoing, "ctx", 0, 0, tiled=True)
    keys = triple[:, 1].reshape(-1, HDIM)
    values = triple[:, 2].reshape(-1, HDIM)
    inv_root = 1.0 / jnp.sqrt(jnp.float32(HDIM))

    def one_block(query):
        scores = jnp.dot(query, keys.T, preferred_element_type=jnp.float32) * inv_root
        best = jnp.maximum(jnp.float32(-1e30), jnp.max(scores, -1))
        probs = jnp.exp(scores - best[:, None])
        denom = jnp.sum(probs, -1)
        accum = jnp.dot(probs.astype(jnp.bfloat16), values, preferred_element_type=jnp.float32)
        return (accum / denom[:, None]).astype(jnp.bfloat16)

    queries = triple[:, 0]
    chunks = 16
    attended = lax.map(one_block, queries.reshape(chunks, -1, HDIM)).reshape(queries.shape)
    by_head = lax.all_to_all(attended, "ctx", 0, 0, tiled=True)[:heads_here]
    return by_head.transpose(1, 0, 2).reshape(group_rows, heads_here * HDIM)


def solution(mesh):
    return jax.shard_map(
        shards,
        mesh=mesh,
        in_specs=(
            P("dp", "head", "ctx"),
            P("dp", "head", "ctx"),
            P(),
            P(),
            P(),
            P(None, ("head", "ctx")),
            P("dp"),
            P(None, ("head", "ctx")),
            P("ctx", "head", None, None),
        ),
        out_specs=P(("dp", "ctx"), "head"),
        check_vma=False,
    )
```

```python
import jax
import jax.numpy as jnp
from jax import lax
from jax.sharding import PartitionSpec as P

D = 5120
HDIM = 128
FREQ = 256


def with_halo(cells, sides, width):
    for axis, dim in sides:
        count = lax.axis_size(axis)
        ends = count - 1
        head = lax.slice_in_dim(cells, 0, width, axis=dim)
        tail = lax.slice_in_dim(cells, cells.shape[dim] - width, cells.shape[dim], axis=dim)
        cells = jnp.concatenate(
            [
                lax.ppermute(tail, axis, [(i, (i + 1) % count) for i in range(ends)]),
                cells,
                lax.ppermute(head, axis, [((i + 1) % count, i) for i in range(ends)]),
            ],
            axis=dim,
        )
    return cells


def gather_rows(cells, axis):
    count = lax.axis_size(axis)
    me = lax.axis_index(axis)
    parts = [cells] + [
        lax.ppermute(cells, axis, [(i, (i + s) % count) for i in range(count)])
        for s in range(1, count)
    ]
    stacked = jnp.stack(parts)
    return jnp.take(stacked, (me - jnp.arange(count)) % count, axis=0)


def split3(value):
    parts = []
    rest = value
    for _ in range(3):
        part = lax.reduce_precision(rest, exponent_bits=8, mantissa_bits=7)
        parts.append(part.astype(jnp.bfloat16))
        rest = rest - part
    return jnp.stack(parts)


def join3(parts):
    return (parts[0].astype(jnp.float32) + parts[1].astype(jnp.float32)) + parts[2].astype(jnp.float32)


def silu_act(value):
    return value * jax.nn.sigmoid(value)


def shards(
    video,
    cache,
    conv_weight,
    conv_bias,
    down_weight,
    patch_weight,
    step_index,
    mod_weight,
    qkv_weight,
):
    cin = conv_weight.shape[2] // 3
    cmid = conv_weight.shape[3]
    frame_count = video.shape[0]
    tile_rows = video.shape[1]
    tile_cols = video.shape[2] // cin
    n_ctx = lax.axis_size("ctx")
    c_idx = lax.axis_index("ctx")
    heads_here = qkv_weight.shape[1]
    out_cols = heads_here * 3 * HDIM
    local = qkv_weight.reshape(qkv_weight.shape[0], out_cols)
    rows = local.shape[0]
    half_rows = rows // 2
    quarter_rows = half_rows // 2
    core = lax.axis_index("dp") % 2
    mine = lax.dynamic_slice_in_dim(local, core * half_rows, half_rows, 0)
    n_dp = lax.axis_size("dp")

    def send(cells, step):
        return lax.ppermute(cells, "ctx", [(i, step(i)) for i in range(n_ctx)])

    def swap(cells):
        return lax.ppermute(cells, "dp", [(i, i ^ 1) for i in range(n_dp)])

    up = lambda i: (i + 2) % n_ctx
    down = lambda i: (i + n_ctx - 2) % n_ctx
    across = lambda i: i ^ 1
    from_up = (c_idx + n_ctx - 2) % n_ctx
    from_down = (c_idx + 2) % n_ctx
    opposite = (c_idx + 4) % n_ctx
    a_up = send(mine, up)
    a_down = send(mine, down)
    a_across = send(mine, across)
    b_up = send(a_up[:quarter_rows], up)
    b_down = send(a_down[quarter_rows:], down)
    b_across_up = send(a_across, up)
    b_across_down = send(a_across, down)
    c_first = send(b_up, across)
    c_second = send(b_down, across)
    stages = [
        [(a_up, from_up, 0), (a_down, from_down, 0), (a_across, c_idx ^ 1, 0)],
        [(b_up, opposite, 0), (b_down, opposite, quarter_rows),
         (b_across_up, from_up ^ 1, 0), (b_across_down, from_down ^ 1, 0)],
        [(c_first, opposite ^ 1, 0), (c_second, opposite ^ 1, quarter_rows)],
    ]
    stages = [
        (stage, ours, swap(ours))
        for stage, ours in ((s, jnp.concatenate([cells for cells, _, _ in s], 0)) for s in stages)
    ]
    frames = jnp.concatenate([cache, video], 0).reshape(frame_count + 2, tile_rows, tile_cols, cin)
    padded = with_halo(frames, (("head", 1), ("ctx", 2)), 1)
    total = jnp.zeros((frame_count, tile_rows, tile_cols, cmid), jnp.float32)
    for time_tap in range(3):
        for row_tap in range(3):
            slab = padded[time_tap : time_tap + frame_count, row_tap : row_tap + tile_rows]
            stacked = jnp.concatenate(
                [slab[:, :, col_tap : col_tap + tile_cols] for col_tap in range(3)], -1
            )
            total = total + jnp.einsum(
                "fyxc,cd->fyxd",
                stacked,
                conv_weight[time_tap, row_tap],
                preferred_element_type=jnp.float32,
            )
    hidden = silu_act(total + conv_bias).astype(jnp.bfloat16)
    stacked = (
        hidden.reshape(frame_count, tile_rows // 2, 2, tile_cols // 2, 2, cmid)
        .transpose(0, 1, 3, 2, 4, 5)
        .reshape(-1, 4 * cmid)
    )
    reduced = silu_act(jnp.dot(stacked, down_weight, preferred_element_type=jnp.float32)).astype(
        jnp.bfloat16
    )
    reduced = reduced.reshape(frame_count, tile_rows // 2, tile_cols // 2, cmid)
    patches = reduced.reshape(frame_count, tile_rows // 4, 2, tile_cols // 4, 2, cmid).transpose(
        0, 1, 3, 2, 4, 5
    )
    patches = patches.reshape(-1, 4 * cmid)
    half = FREQ // 2
    freqs = jnp.exp(-jnp.log(10000.0) * jnp.arange(half, dtype=jnp.float32) / half)
    angles = step_index[0].astype(jnp.float32) * freqs
    timing = jnp.concatenate([jnp.cos(angles), jnp.sin(angles)]).astype(jnp.bfloat16)
    mod_share = jnp.dot(timing[None, :], mod_weight, preferred_element_type=jnp.float32)[0]
    n_head = lax.axis_size("head")
    n_ctx = lax.axis_size("ctx")
    h_idx = lax.axis_index("head")
    c_idx = lax.axis_index("ctx")
    quarter = D // n_head
    share_width = patch_weight.shape[1]
    share_parts = split3(mod_share).reshape(-1, share_width)
    carried = lax.all_gather(
        jnp.concatenate([patch_weight, share_parts], 0), "ctx", axis=1, tiled=True
    )
    weight_quarter = carried[: patch_weight.shape[0]]
    row_share = (
        carried[patch_weight.shape[0] :]
        .reshape(-1, n_ctx, share_width)
        .transpose(1, 0, 2)
        .reshape(n_ctx, 3, -1)
        .transpose(1, 0, 2)
        .reshape(3, -1)
    )
    row_parts = join3(row_share)
    block_patches = gather_rows(patches, "head").reshape(-1, patches.shape[1])
    embedded = jnp.dot(block_patches, weight_quarter, preferred_element_type=jnp.float32)
    token_count = embedded.shape[0]
    riding = gather_rows(jnp.concatenate([jnp.sum(embedded * embedded, -1), row_parts]), "head")
    squares = riding[:, :token_count]
    modulation = riding[:, token_count:].reshape(-1)
    scale = lax.dynamic_slice_in_dim(modulation, h_idx * quarter, quarter)
    shift = lax.dynamic_slice_in_dim(modulation, D + h_idx * quarter, quarter)
    inverse = lax.rsqrt(jnp.sum(squares, 0) / D + 1e-06)[:, None]
    normed_quarter = (embedded * inverse * (1.0 + scale) + shift).astype(jnp.bfloat16)
    normed = lax.all_gather(normed_quarter, "head", axis=1, tiled=True)
    group_rows = normed.shape[0]
    heads_here = qkv_weight.shape[1]
    out_cols = heads_here * 3 * HDIM
    qkv = None
    for number, (stage, ours, theirs) in enumerate(stages):
        weights = [local] if number == 0 else []
        columns = [lax.dynamic_slice_in_dim(normed, c_idx * rows, rows, 1)] if number == 0 else []
        weights += [ours, theirs]
        for side in (core, 1 - core):
            for cells, block, offset in stage:
                columns.append(
                    lax.dynamic_slice_in_dim(
                        normed, block * rows + side * half_rows + offset, cells.shape[0], 1
                    )
                )
        part = jnp.dot(
            jnp.concatenate(columns, 1),
            jnp.concatenate(weights, 0),
            preferred_element_type=jnp.float32,
        )
        qkv = part if qkv is None else qkv + part
    qkv = qkv.astype(jnp.bfloat16).reshape(group_rows, heads_here, 3, HDIM)
    active = min(heads_here, n_ctx)
    spare = n_ctx - active
    by_part = qkv.transpose(1, 2, 0, 3)
    outgoing = jnp.concatenate([by_part, jnp.zeros((spare,) + by_part.shape[1:], qkv.dtype)], 0)
    triple = lax.all_to_all(outgoing, "ctx", 0, 0, tiled=True)
    keys = triple[:, 1].reshape(-1, HDIM)
    values = triple[:, 2].reshape(-1, HDIM)
    inv_root = 1.0 / jnp.sqrt(jnp.float32(HDIM))

    def one_block(query):
        scores = jnp.dot(query, keys.T, preferred_element_type=jnp.float32) * inv_root
        best = jnp.maximum(jnp.float32(-1e30), jnp.max(scores, -1))
        probs = jnp.exp(scores - best[:, None])
        denom = jnp.sum(probs, -1)
        accum = jnp.dot(probs.astype(jnp.bfloat16), values, preferred_element_type=jnp.float32)
        return (accum / denom[:, None]).astype(jnp.bfloat16)

    attended = jnp.stack([one_block(triple[s, 0]) for s in range(triple.shape[0])])
    by_head = lax.all_to_all(attended, "ctx", 0, 0, tiled=True)[:heads_here]
    return by_head.transpose(1, 0, 2).reshape(group_rows, heads_here * HDIM)


def solution(mesh):
    return jax.shard_map(
        shards,
        mesh=mesh,
        in_specs=(
            P("dp", "head", "ctx"),
            P("dp", "head", "ctx"),
            P(),
            P(),
            P(),
            P(None, ("head", "ctx")),
            P("dp"),
            P(None, ("head", "ctx")),
            P("ctx", "head", None, None),
        ),
        out_specs=P(("dp", "ctx"), "head"),
        check_vma=False,
    )
```

```python
import jax
import jax.numpy as jnp
from jax import lax
from jax.sharding import PartitionSpec as P

D = 5120
HDIM = 128
FREQ = 256


def with_halo(cells, sides, width):
    for axis, dim in sides:
        count = lax.axis_size(axis)
        ends = count - 1
        head = lax.slice_in_dim(cells, 0, width, axis=dim)
        tail = lax.slice_in_dim(cells, cells.shape[dim] - width, cells.shape[dim], axis=dim)
        cells = jnp.concatenate(
            [
                lax.ppermute(tail, axis, [(i, (i + 1) % count) for i in range(ends)]),
                cells,
                lax.ppermute(head, axis, [((i + 1) % count, i) for i in range(ends)]),
            ],
            axis=dim,
        )
    return cells


def gather_rows(cells, axis):
    count = lax.axis_size(axis)
    me = lax.axis_index(axis)
    parts = [cells] + [
        lax.ppermute(cells, axis, [(i, (i + s) % count) for i in range(count)])
        for s in range(1, count)
    ]
    stacked = jnp.stack(parts)
    return jnp.take(stacked, (me - jnp.arange(count)) % count, axis=0)


def split3(value):
    parts = []
    rest = value
    for _ in range(3):
        part = lax.reduce_precision(rest, exponent_bits=8, mantissa_bits=7)
        parts.append(part.astype(jnp.bfloat16))
        rest = rest - part
    return jnp.stack(parts)


def join3(parts):
    return (parts[0].astype(jnp.float32) + parts[1].astype(jnp.float32)) + parts[2].astype(jnp.float32)


def silu_act(value):
    return value * jax.nn.sigmoid(value)


def shards(
    video,
    cache,
    conv_weight,
    conv_bias,
    down_weight,
    patch_weight,
    step_index,
    mod_weight,
    qkv_weight,
):
    cin = conv_weight.shape[2] // 3
    cmid = conv_weight.shape[3]
    frame_count = video.shape[0]
    tile_rows = video.shape[1]
    tile_cols = video.shape[2] // cin
    n_ctx = lax.axis_size("ctx")
    c_idx = lax.axis_index("ctx")
    heads_here = qkv_weight.shape[1]
    out_cols = heads_here * 3 * HDIM
    local = qkv_weight.reshape(qkv_weight.shape[0], out_cols)
    rows = local.shape[0]
    half_rows = rows // 2
    quarter_rows = half_rows // 2
    core = lax.axis_index("dp") % 2
    mine = lax.dynamic_slice_in_dim(local, core * half_rows, half_rows, 0)
    n_dp = lax.axis_size("dp")

    def send(cells, step):
        return lax.ppermute(cells, "ctx", [(i, step(i)) for i in range(n_ctx)])

    def swap(cells):
        return lax.ppermute(cells, "dp", [(i, i ^ 1) for i in range(n_dp)])

    up = lambda i: (i + 2) % n_ctx
    down = lambda i: (i + n_ctx - 2) % n_ctx
    across = lambda i: i ^ 1
    from_up = (c_idx + n_ctx - 2) % n_ctx
    from_down = (c_idx + 2) % n_ctx
    opposite = (c_idx + 4) % n_ctx
    a_up = send(mine, up)
    a_down = send(mine, down)
    a_across = send(mine, across)
    b_up = send(a_up[:quarter_rows], up)
    b_down = send(a_down[quarter_rows:], down)
    b_across_up = send(a_across, up)
    b_across_down = send(a_across, down)
    c_first = send(b_up, across)
    c_second = send(b_down, across)
    stages = [
        [(a_up, from_up, 0), (a_down, from_down, 0), (a_across, c_idx ^ 1, 0)],
        [(b_up, opposite, 0), (b_down, opposite, quarter_rows),
         (b_across_up, from_up ^ 1, 0), (b_across_down, from_down ^ 1, 0)],
        [(c_first, opposite ^ 1, 0), (c_second, opposite ^ 1, quarter_rows)],
    ]
    stages = [
        (stage, ours, swap(ours))
        for stage, ours in ((s, jnp.concatenate([cells for cells, _, _ in s], 0)) for s in stages)
    ]
    frames = jnp.concatenate([cache, video], 0).reshape(frame_count + 2, tile_rows, tile_cols, cin)
    padded = with_halo(frames, (("head", 1), ("ctx", 2)), 1)
    total = jnp.zeros((frame_count, tile_rows, tile_cols, cmid), jnp.float32)
    for time_tap in range(3):
        for row_tap in range(3):
            slab = padded[time_tap : time_tap + frame_count, row_tap : row_tap + tile_rows]
            stacked = jnp.concatenate(
                [slab[:, :, col_tap : col_tap + tile_cols] for col_tap in range(3)], -1
            )
            total = total + jnp.einsum(
                "fyxc,cd->fyxd",
                stacked,
                conv_weight[time_tap, row_tap],
                preferred_element_type=jnp.float32,
            )
    hidden = silu_act(total + conv_bias).astype(jnp.bfloat16)
    stacked = (
        hidden.reshape(frame_count, tile_rows // 2, 2, tile_cols // 2, 2, cmid)
        .transpose(0, 1, 3, 2, 4, 5)
        .reshape(-1, 4 * cmid)
    )
    reduced = silu_act(jnp.dot(stacked, down_weight, preferred_element_type=jnp.float32)).astype(
        jnp.bfloat16
    )
    reduced = reduced.reshape(frame_count, tile_rows // 2, tile_cols // 2, cmid)
    patches = reduced.reshape(frame_count, tile_rows // 4, 2, tile_cols // 4, 2, cmid).transpose(
        0, 1, 3, 2, 4, 5
    )
    patches = patches.reshape(-1, 4 * cmid)
    half = FREQ // 2
    freqs = jnp.exp(-jnp.log(10000.0) * jnp.arange(half, dtype=jnp.float32) / half)
    angles = step_index[0].astype(jnp.float32) * freqs
    timing = jnp.concatenate([jnp.cos(angles), jnp.sin(angles)]).astype(jnp.bfloat16)
    mod_share = jnp.dot(timing[None, :], mod_weight, preferred_element_type=jnp.float32)[0]
    n_head = lax.axis_size("head")
    n_ctx = lax.axis_size("ctx")
    h_idx = lax.axis_index("head")
    c_idx = lax.axis_index("ctx")
    quarter = D // n_head
    share_width = patch_weight.shape[1]
    share_parts = split3(mod_share).reshape(-1, share_width)
    carried = lax.all_gather(
        jnp.concatenate([patch_weight, share_parts], 0), "ctx", axis=1, tiled=True
    )
    weight_quarter = carried[: patch_weight.shape[0]]
    row_share = (
        carried[patch_weight.shape[0] :]
        .reshape(-1, n_ctx, share_width)
        .transpose(1, 0, 2)
        .reshape(n_ctx, 3, -1)
        .transpose(1, 0, 2)
        .reshape(3, -1)
    )
    row_parts = join3(row_share)
    block_patches = gather_rows(patches, "head").reshape(-1, patches.shape[1])
    embedded = jnp.dot(block_patches, weight_quarter, preferred_element_type=jnp.float32)
    token_count = embedded.shape[0]
    riding = gather_rows(jnp.concatenate([jnp.sum(embedded * embedded, -1), row_parts]), "head")
    squares = riding[:, :token_count]
    modulation = riding[:, token_count:].reshape(-1)
    scale = lax.dynamic_slice_in_dim(modulation, h_idx * quarter, quarter)
    shift = lax.dynamic_slice_in_dim(modulation, D + h_idx * quarter, quarter)
    inverse = lax.rsqrt(jnp.sum(squares, 0) / D + 1e-06)[:, None]
    normed_quarter = (embedded * inverse * (1.0 + scale) + shift).astype(jnp.bfloat16)
    normed = lax.all_gather(normed_quarter, "head", axis=1, tiled=True)
    group_rows = normed.shape[0]
    heads_here = qkv_weight.shape[1]
    out_cols = heads_here * 3 * HDIM
    qkv = None
    for number, (stage, ours, theirs) in enumerate(stages):
        weights = [local] if number == 0 else []
        columns = [lax.dynamic_slice_in_dim(normed, c_idx * rows, rows, 1)] if number == 0 else []
        weights += [ours, theirs]
        for side in (core, 1 - core):
            for cells, block, offset in stage:
                columns.append(
                    lax.dynamic_slice_in_dim(
                        normed, block * rows + side * half_rows + offset, cells.shape[0], 1
                    )
                )
        part = jnp.dot(
            jnp.concatenate(columns, 1),
            jnp.concatenate(weights, 0),
            preferred_element_type=jnp.float32,
        )
        qkv = part if qkv is None else qkv + part
    qkv = qkv.astype(jnp.bfloat16).reshape(group_rows, heads_here, 3, HDIM)
    active = min(heads_here, n_ctx)
    received = [lax.dynamic_index_in_dim(qkv, jnp.minimum(c_idx, active - 1), 1, keepdims=False)]
    for s in range(1, n_ctx):
        target = jnp.minimum((c_idx + s) % n_ctx, active - 1)
        received.append(
            lax.ppermute(
                lax.dynamic_index_in_dim(qkv, target, 1, keepdims=False),
                "ctx",
                [(b, (b + s) % n_ctx) for b in range(n_ctx) if (b + s) % n_ctx < active],
            )
        )
    triple = jnp.stack(received)
    keys = triple[:, :, 1].reshape(-1, HDIM)
    values = triple[:, :, 2].reshape(-1, HDIM)
    inv_root = 1.0 / jnp.sqrt(jnp.float32(HDIM))

    def one_block(query):
        scores = jnp.dot(query, keys.T, preferred_element_type=jnp.float32) * inv_root
        best = jnp.maximum(jnp.float32(-1e30), jnp.max(scores, -1))
        probs = jnp.exp(scores - best[:, None])
        denom = jnp.sum(probs, -1)
        accum = jnp.dot(probs.astype(jnp.bfloat16), values, preferred_element_type=jnp.float32)
        return (accum / denom[:, None]).astype(jnp.bfloat16)

    attended = lax.map(one_block, triple[:, :, 0])
    attended = jnp.take(attended, (c_idx - jnp.arange(n_ctx)) % n_ctx, axis=0)
    by_head = lax.all_to_all(attended, "ctx", 0, 0, tiled=True)[:heads_here]
    return by_head.transpose(1, 0, 2).reshape(group_rows, heads_here * HDIM)


def solution(mesh):
    return jax.shard_map(
        shards,
        mesh=mesh,
        in_specs=(
            P("dp", "head", "ctx"),
            P("dp", "head", "ctx"),
            P(),
            P(),
            P(),
            P(None, ("head", "ctx")),
            P("dp"),
            P(None, ("head", "ctx")),
            P("ctx", "head", None, None),
        ),
        out_specs=P(("dp", "ctx"), "head"),
        check_vma=False,
    )
```

```python
import jax
import jax.numpy as jnp
from jax import lax
from jax.sharding import PartitionSpec as P

D = 5120
HDIM = 128
FREQ = 256


def with_halo(cells, sides, width):
    for axis, dim in sides:
        count = lax.axis_size(axis)
        ends = count - 1
        head = lax.slice_in_dim(cells, 0, width, axis=dim)
        tail = lax.slice_in_dim(cells, cells.shape[dim] - width, cells.shape[dim], axis=dim)
        cells = jnp.concatenate(
            [
                lax.ppermute(tail, axis, [(i, (i + 1) % count) for i in range(ends)]),
                cells,
                lax.ppermute(head, axis, [((i + 1) % count, i) for i in range(ends)]),
            ],
            axis=dim,
        )
    return cells


def gather_rows(cells, axis):
    count = lax.axis_size(axis)
    me = lax.axis_index(axis)
    parts = [cells] + [
        lax.ppermute(cells, axis, [(i, (i + s) % count) for i in range(count)])
        for s in range(1, count)
    ]
    stacked = jnp.stack(parts)
    return jnp.take(stacked, (me - jnp.arange(count)) % count, axis=0)


def split3(value):
    parts = []
    rest = value
    for _ in range(3):
        part = lax.reduce_precision(rest, exponent_bits=8, mantissa_bits=7)
        parts.append(part.astype(jnp.bfloat16))
        rest = rest - part
    return jnp.stack(parts)


def join3(parts):
    return (parts[0].astype(jnp.float32) + parts[1].astype(jnp.float32)) + parts[2].astype(jnp.float32)


def silu_act(value):
    return value * jax.nn.sigmoid(value)


def shards(
    video,
    cache,
    conv_weight,
    conv_bias,
    down_weight,
    patch_weight,
    step_index,
    mod_weight,
    qkv_weight,
):
    cin = conv_weight.shape[2] // 3
    cmid = conv_weight.shape[3]
    frame_count = video.shape[0]
    tile_rows = video.shape[1]
    tile_cols = video.shape[2] // cin
    n_ctx = lax.axis_size("ctx")
    c_idx = lax.axis_index("ctx")
    heads_here = qkv_weight.shape[1]
    out_cols = heads_here * 3 * HDIM
    local = qkv_weight.reshape(qkv_weight.shape[0], out_cols)
    rows = local.shape[0]
    half_rows = rows // 2
    quarter_rows = half_rows // 2
    core = lax.axis_index("dp") % 2
    mine = lax.dynamic_slice_in_dim(local, core * half_rows, half_rows, 0)
    n_dp = lax.axis_size("dp")

    def send(cells, step):
        return lax.ppermute(cells, "ctx", [(i, step(i)) for i in range(n_ctx)])

    def swap(cells):
        return lax.ppermute(cells, "dp", [(i, i ^ 1) for i in range(n_dp)])

    up = lambda i: (i + 2) % n_ctx
    down = lambda i: (i + n_ctx - 2) % n_ctx
    across = lambda i: i ^ 1
    from_up = (c_idx + n_ctx - 2) % n_ctx
    from_down = (c_idx + 2) % n_ctx
    opposite = (c_idx + 4) % n_ctx
    a_up = send(mine, up)
    a_down = send(mine, down)
    a_across = send(mine, across)
    b_up = send(a_up[:quarter_rows], up)
    b_down = send(a_down[quarter_rows:], down)
    b_across_up = send(a_across, up)
    b_across_down = send(a_across, down)
    c_first = send(b_up, across)
    c_second = send(b_down, across)
    stages = [
        [(a_up, from_up, 0), (a_down, from_down, 0), (a_across, c_idx ^ 1, 0)],
        [(b_up, opposite, 0), (b_down, opposite, quarter_rows),
         (b_across_up, from_up ^ 1, 0), (b_across_down, from_down ^ 1, 0)],
        [(c_first, opposite ^ 1, 0), (c_second, opposite ^ 1, quarter_rows)],
    ]
    stages = [
        (stage, ours, swap(ours))
        for stage, ours in ((s, jnp.concatenate([cells for cells, _, _ in s], 0)) for s in stages)
    ]
    frames = jnp.concatenate([cache, video], 0).reshape(frame_count + 2, tile_rows, tile_cols, cin)
    padded = with_halo(frames, (("head", 1), ("ctx", 2)), 1)
    total = jnp.zeros((frame_count, tile_rows, tile_cols, cmid), jnp.float32)
    for time_tap in range(3):
        for row_tap in range(3):
            slab = padded[time_tap : time_tap + frame_count, row_tap : row_tap + tile_rows]
            stacked = jnp.concatenate(
                [slab[:, :, col_tap : col_tap + tile_cols] for col_tap in range(3)], -1
            )
            total = total + jnp.einsum(
                "fyxc,cd->fyxd",
                stacked,
                conv_weight[time_tap, row_tap],
                preferred_element_type=jnp.float32,
            )
    hidden = silu_act(total + conv_bias).astype(jnp.bfloat16)
    stacked = (
        hidden.reshape(frame_count, tile_rows // 2, 2, tile_cols // 2, 2, cmid)
        .transpose(0, 1, 3, 2, 4, 5)
        .reshape(-1, 4 * cmid)
    )
    reduced = silu_act(jnp.dot(stacked, down_weight, preferred_element_type=jnp.float32)).astype(
        jnp.bfloat16
    )
    reduced = reduced.reshape(frame_count, tile_rows // 2, tile_cols // 2, cmid)
    patches = reduced.reshape(frame_count, tile_rows // 4, 2, tile_cols // 4, 2, cmid).transpose(
        0, 1, 3, 2, 4, 5
    )
    patches = patches.reshape(-1, 4 * cmid)
    half = FREQ // 2
    freqs = jnp.exp(-jnp.log(10000.0) * jnp.arange(half, dtype=jnp.float32) / half)
    angles = step_index[0].astype(jnp.float32) * freqs
    timing = jnp.concatenate([jnp.cos(angles), jnp.sin(angles)]).astype(jnp.bfloat16)
    mod_share = jnp.dot(timing[None, :], mod_weight, preferred_element_type=jnp.float32)[0]
    n_head = lax.axis_size("head")
    n_ctx = lax.axis_size("ctx")
    h_idx = lax.axis_index("head")
    c_idx = lax.axis_index("ctx")
    quarter = D // n_head
    share_width = patch_weight.shape[1]
    share_parts = split3(mod_share).reshape(-1, share_width)
    carried = lax.all_gather(
        jnp.concatenate([patch_weight, share_parts], 0), "ctx", axis=1, tiled=True
    )
    weight_quarter = carried[: patch_weight.shape[0]]
    row_share = (
        carried[patch_weight.shape[0] :]
        .reshape(-1, n_ctx, share_width)
        .transpose(1, 0, 2)
        .reshape(n_ctx, 3, -1)
        .transpose(1, 0, 2)
        .reshape(3, -1)
    )
    row_parts = join3(row_share)
    block_patches = gather_rows(patches, "head").reshape(-1, patches.shape[1])
    embedded = jnp.dot(block_patches, weight_quarter, preferred_element_type=jnp.float32)
    token_count = embedded.shape[0]
    riding = gather_rows(jnp.concatenate([jnp.sum(embedded * embedded, -1), row_parts]), "head")
    squares = riding[:, :token_count]
    modulation = riding[:, token_count:].reshape(-1)
    scale = lax.dynamic_slice_in_dim(modulation, h_idx * quarter, quarter)
    shift = lax.dynamic_slice_in_dim(modulation, D + h_idx * quarter, quarter)
    inverse = lax.rsqrt(jnp.sum(squares, 0) / D + 1e-06)[:, None]
    normed_quarter = (embedded * inverse * (1.0 + scale) + shift).astype(jnp.bfloat16)
    normed = lax.all_gather(normed_quarter, "head", axis=1, tiled=True)
    group_rows = normed.shape[0]
    heads_here = qkv_weight.shape[1]
    out_cols = heads_here * 3 * HDIM
    qkv = None
    for number, (stage, ours, theirs) in enumerate(stages):
        weights = [local] if number == 0 else []
        columns = [lax.dynamic_slice_in_dim(normed, c_idx * rows, rows, 1)] if number == 0 else []
        weights += [ours, theirs]
        for side in (core, 1 - core):
            for cells, block, offset in stage:
                columns.append(
                    lax.dynamic_slice_in_dim(
                        normed, block * rows + side * half_rows + offset, cells.shape[0], 1
                    )
                )
        part = jnp.dot(
            jnp.concatenate(columns, 1),
            jnp.concatenate(weights, 0),
            preferred_element_type=jnp.float32,
        )
        qkv = part if qkv is None else qkv + part
    qkv = qkv.astype(jnp.bfloat16).reshape(group_rows, heads_here, 3, HDIM)
    active = min(heads_here, n_ctx)
    spare = n_ctx - active
    by_head = qkv.transpose(1, 0, 2, 3)
    outgoing = jnp.concatenate([by_head, jnp.zeros((spare,) + by_head.shape[1:], qkv.dtype)], 0)
    triple = lax.all_to_all(outgoing.reshape(n_ctx, -1), "ctx", 0, 0, tiled=True).reshape(outgoing.shape)
    keys = triple[:, :, 1].reshape(-1, HDIM)
    values = triple[:, :, 2].reshape(-1, HDIM)
    inv_root = 1.0 / jnp.sqrt(jnp.float32(HDIM))

    def one_block(query):
        scores = jnp.dot(query, keys.T, preferred_element_type=jnp.float32) * inv_root
        best = jnp.maximum(jnp.float32(-1e30), jnp.max(scores, -1))
        probs = jnp.exp(scores - best[:, None])
        denom = jnp.sum(probs, -1)
        accum = jnp.dot(probs.astype(jnp.bfloat16), values, preferred_element_type=jnp.float32)
        return (accum / denom[:, None]).astype(jnp.bfloat16)

    attended = lax.map(one_block, triple[:, :, 0])
    by_head = lax.all_to_all(attended, "ctx", 0, 0, tiled=True)[:heads_here]
    return by_head.transpose(1, 0, 2).reshape(group_rows, heads_here * HDIM)


def solution(mesh):
    return jax.shard_map(
        shards,
        mesh=mesh,
        in_specs=(
            P("dp", "head", "ctx"),
            P("dp", "head", "ctx"),
            P(),
            P(),
            P(),
            P(None, ("head", "ctx")),
            P("dp"),
            P(None, ("head", "ctx")),
            P("ctx", "head", None, None),
        ),
        out_specs=P(("dp", "ctx"), "head"),
        check_vma=False,
    )
```

```python
import jax
import jax.numpy as jnp
from jax import lax
from jax.sharding import PartitionSpec as P

D = 5120
HDIM = 128
FREQ = 256


def with_halo(cells, sides, width):
    for axis, dim in sides:
        count = lax.axis_size(axis)
        ends = count - 1
        head = lax.slice_in_dim(cells, 0, width, axis=dim)
        tail = lax.slice_in_dim(cells, cells.shape[dim] - width, cells.shape[dim], axis=dim)
        cells = jnp.concatenate(
            [
                lax.ppermute(tail, axis, [(i, (i + 1) % count) for i in range(ends)]),
                cells,
                lax.ppermute(head, axis, [((i + 1) % count, i) for i in range(ends)]),
            ],
            axis=dim,
        )
    return cells


def gather_rows(cells, axis):
    count = lax.axis_size(axis)
    me = lax.axis_index(axis)
    parts = [cells] + [
        lax.ppermute(cells, axis, [(i, (i + s) % count) for i in range(count)])
        for s in range(1, count)
    ]
    stacked = jnp.stack(parts)
    return jnp.take(stacked, (me - jnp.arange(count)) % count, axis=0)


def split3(value):
    parts = []
    rest = value
    for _ in range(3):
        part = lax.reduce_precision(rest, exponent_bits=8, mantissa_bits=7)
        parts.append(part.astype(jnp.bfloat16))
        rest = rest - part
    return jnp.stack(parts)


def join3(parts):
    return (parts[0].astype(jnp.float32) + parts[1].astype(jnp.float32)) + parts[2].astype(jnp.float32)


def silu_act(value):
    return value * jax.nn.sigmoid(value)


def shards(
    video,
    cache,
    conv_weight,
    conv_bias,
    down_weight,
    patch_weight,
    step_index,
    mod_weight,
    qkv_weight,
):
    cin = conv_weight.shape[2] // 3
    cmid = conv_weight.shape[3]
    frame_count = video.shape[0]
    tile_rows = video.shape[1]
    tile_cols = video.shape[2] // cin
    n_ctx = lax.axis_size("ctx")
    c_idx = lax.axis_index("ctx")
    heads_here = qkv_weight.shape[1]
    out_cols = heads_here * 3 * HDIM
    local = qkv_weight.reshape(qkv_weight.shape[0], out_cols)
    rows = local.shape[0]
    half_rows = rows // 2
    quarter_rows = half_rows // 2
    core = lax.axis_index("dp") % 2
    mine = lax.dynamic_slice_in_dim(local, core * half_rows, half_rows, 0)
    n_dp = lax.axis_size("dp")

    def send(cells, step):
        return lax.ppermute(cells, "ctx", [(i, step(i)) for i in range(n_ctx)])

    def swap(cells):
        return lax.ppermute(cells, "dp", [(i, i ^ 1) for i in range(n_dp)])

    up = lambda i: (i + 2) % n_ctx
    down = lambda i: (i + n_ctx - 2) % n_ctx
    across = lambda i: i ^ 1
    from_up = (c_idx + n_ctx - 2) % n_ctx
    from_down = (c_idx + 2) % n_ctx
    opposite = (c_idx + 4) % n_ctx
    a_up = send(mine, up)
    a_down = send(mine, down)
    a_across = send(mine, across)
    b_up = send(a_up[:quarter_rows], up)
    b_down = send(a_down[quarter_rows:], down)
    b_across_up = send(a_across, up)
    b_across_down = send(a_across, down)
    c_first = send(b_up, across)
    c_second = send(b_down, across)
    stages = [
        [(a_up, from_up, 0), (a_down, from_down, 0), (a_across, c_idx ^ 1, 0)],
        [(b_up, opposite, 0), (b_down, opposite, quarter_rows),
         (b_across_up, from_up ^ 1, 0), (b_across_down, from_down ^ 1, 0)],
        [(c_first, opposite ^ 1, 0), (c_second, opposite ^ 1, quarter_rows)],
    ]
    stages = [
        (stage, ours, swap(ours))
        for stage, ours in ((s, jnp.concatenate([cells for cells, _, _ in s], 0)) for s in stages)
    ]
    frames = jnp.concatenate([cache, video], 0).reshape(frame_count + 2, tile_rows, tile_cols, cin)
    padded = with_halo(frames, (("head", 1), ("ctx", 2)), 1)
    total = jnp.zeros((frame_count, tile_rows, tile_cols, cmid), jnp.float32)
    for time_tap in range(3):
        for row_tap in range(3):
            slab = padded[time_tap : time_tap + frame_count, row_tap : row_tap + tile_rows]
            stacked = jnp.concatenate(
                [slab[:, :, col_tap : col_tap + tile_cols] for col_tap in range(3)], -1
            )
            total = total + jnp.einsum(
                "fyxc,cd->fyxd",
                stacked,
                conv_weight[time_tap, row_tap],
                preferred_element_type=jnp.float32,
            )
    hidden = silu_act(total + conv_bias).astype(jnp.bfloat16)
    stacked = (
        hidden.reshape(frame_count, tile_rows // 2, 2, tile_cols // 2, 2, cmid)
        .transpose(0, 1, 3, 2, 4, 5)
        .reshape(-1, 4 * cmid)
    )
    reduced = silu_act(jnp.dot(stacked, down_weight, preferred_element_type=jnp.float32)).astype(
        jnp.bfloat16
    )
    reduced = reduced.reshape(frame_count, tile_rows // 2, tile_cols // 2, cmid)
    patches = reduced.reshape(frame_count, tile_rows // 4, 2, tile_cols // 4, 2, cmid).transpose(
        0, 1, 3, 2, 4, 5
    )
    patches = patches.reshape(-1, 4 * cmid)
    half = FREQ // 2
    freqs = jnp.exp(-jnp.log(10000.0) * jnp.arange(half, dtype=jnp.float32) / half)
    angles = step_index[0].astype(jnp.float32) * freqs
    timing = jnp.concatenate([jnp.cos(angles), jnp.sin(angles)]).astype(jnp.bfloat16)
    mod_share = jnp.dot(timing[None, :], mod_weight, preferred_element_type=jnp.float32)[0]
    n_head = lax.axis_size("head")
    n_ctx = lax.axis_size("ctx")
    h_idx = lax.axis_index("head")
    c_idx = lax.axis_index("ctx")
    quarter = D // n_head
    share_width = patch_weight.shape[1]
    share_parts = split3(mod_share).reshape(-1, share_width)
    carried = lax.all_gather(
        jnp.concatenate([patch_weight, share_parts], 0), "ctx", axis=1, tiled=True
    )
    weight_quarter = carried[: patch_weight.shape[0]]
    row_share = (
        carried[patch_weight.shape[0] :]
        .reshape(-1, n_ctx, share_width)
        .transpose(1, 0, 2)
        .reshape(n_ctx, 3, -1)
        .transpose(1, 0, 2)
        .reshape(3, -1)
    )
    row_parts = join3(row_share)
    block_patches = gather_rows(patches, "head").reshape(-1, patches.shape[1])
    embedded = jnp.dot(block_patches, weight_quarter, preferred_element_type=jnp.float32)
    token_count = embedded.shape[0]
    riding = gather_rows(jnp.concatenate([jnp.sum(embedded * embedded, -1), row_parts]), "head")
    squares = riding[:, :token_count]
    modulation = riding[:, token_count:].reshape(-1)
    scale = lax.dynamic_slice_in_dim(modulation, h_idx * quarter, quarter)
    shift = lax.dynamic_slice_in_dim(modulation, D + h_idx * quarter, quarter)
    inverse = lax.rsqrt(jnp.sum(squares, 0) / D + 1e-06)[:, None]
    normed_quarter = (embedded * inverse * (1.0 + scale) + shift).astype(jnp.bfloat16)
    normed = lax.all_gather(normed_quarter, "head", axis=1, tiled=True)
    group_rows = normed.shape[0]
    heads_here = qkv_weight.shape[1]
    out_cols = heads_here * 3 * HDIM
    qkv = None
    for number, (stage, ours, theirs) in enumerate(stages):
        weights = [local] if number == 0 else []
        columns = [lax.dynamic_slice_in_dim(normed, c_idx * rows, rows, 1)] if number == 0 else []
        weights += [ours, theirs]
        for side in (core, 1 - core):
            for cells, block, offset in stage:
                columns.append(
                    lax.dynamic_slice_in_dim(
                        normed, block * rows + side * half_rows + offset, cells.shape[0], 1
                    )
                )
        part = jnp.dot(
            jnp.concatenate(columns, 1),
            jnp.concatenate(weights, 0),
            preferred_element_type=jnp.float32,
        )
        qkv = part if qkv is None else qkv + part
    qkv = qkv.astype(jnp.bfloat16).reshape(group_rows, heads_here, 3, HDIM)
    active = min(heads_here, n_ctx)
    spare = n_ctx - active
    by_part = qkv.transpose(1, 2, 0, 3)
    outgoing = jnp.concatenate([by_part, jnp.zeros((spare,) + by_part.shape[1:], qkv.dtype)], 0)
    triple = lax.all_to_all(outgoing, "ctx", 0, 0, tiled=True)
    keys = triple[:, 1].reshape(-1, HDIM)
    values = triple[:, 2].reshape(-1, HDIM)
    inv_root = 1.0 / jnp.sqrt(jnp.float32(HDIM))

    def one_block(query):
        scores = jnp.dot(query, keys.T, preferred_element_type=jnp.float32) * inv_root
        best = jnp.maximum(jnp.float32(-1e30), jnp.max(scores, -1))
        probs = jnp.exp(scores - best[:, None])
        denom = jnp.sum(probs, -1)
        accum = jnp.dot(probs.astype(jnp.bfloat16), values, preferred_element_type=jnp.float32)
        return (accum / denom[:, None]).astype(jnp.bfloat16)

    queries = lax.optimization_barrier(triple[:, 0].reshape(-1, HDIM)).reshape(triple.shape[0], -1, HDIM)
    attended = lax.map(one_block, queries)
    by_head = lax.all_to_all(attended, "ctx", 0, 0, tiled=True)[:heads_here]
    return by_head.transpose(1, 0, 2).reshape(group_rows, heads_here * HDIM)


def solution(mesh):
    return jax.shard_map(
        shards,
        mesh=mesh,
        in_specs=(
            P("dp", "head", "ctx"),
            P("dp", "head", "ctx"),
            P(),
            P(),
            P(),
            P(None, ("head", "ctx")),
            P("dp"),
            P(None, ("head", "ctx")),
            P("ctx", "head", None, None),
        ),
        out_specs=P(("dp", "ctx"), "head"),
        check_vma=False,
    )
```

```python
import jax
import jax.numpy as jnp
from jax import lax
from jax.sharding import PartitionSpec as P

D = 5120
HDIM = 128
FREQ = 256


def with_halo(cells, sides, width):
    for axis, dim in sides:
        count = lax.axis_size(axis)
        ends = count - 1
        head = lax.slice_in_dim(cells, 0, width, axis=dim)
        tail = lax.slice_in_dim(cells, cells.shape[dim] - width, cells.shape[dim], axis=dim)
        cells = jnp.concatenate(
            [
                lax.ppermute(tail, axis, [(i, (i + 1) % count) for i in range(ends)]),
                cells,
                lax.ppermute(head, axis, [((i + 1) % count, i) for i in range(ends)]),
            ],
            axis=dim,
        )
    return cells


def gather_rows(cells, axis):
    count = lax.axis_size(axis)
    me = lax.axis_index(axis)
    parts = [cells] + [
        lax.ppermute(cells, axis, [(i, (i + s) % count) for i in range(count)])
        for s in range(1, count)
    ]
    stacked = jnp.stack(parts)
    return jnp.take(stacked, (me - jnp.arange(count)) % count, axis=0)


def split3(value):
    parts = []
    rest = value
    for _ in range(3):
        part = lax.reduce_precision(rest, exponent_bits=8, mantissa_bits=7)
        parts.append(part.astype(jnp.bfloat16))
        rest = rest - part
    return jnp.stack(parts)


def join3(parts):
    return (parts[0].astype(jnp.float32) + parts[1].astype(jnp.float32)) + parts[2].astype(jnp.float32)


def silu_act(value):
    return value * jax.nn.sigmoid(value)


def shards(
    video,
    cache,
    conv_weight,
    conv_bias,
    down_weight,
    patch_weight,
    step_index,
    mod_weight,
    qkv_weight,
):
    cin = conv_weight.shape[2] // 3
    cmid = conv_weight.shape[3]
    frame_count = video.shape[0]
    tile_rows = video.shape[1]
    tile_cols = video.shape[2] // cin
    n_ctx = lax.axis_size("ctx")
    c_idx = lax.axis_index("ctx")
    heads_here = qkv_weight.shape[1]
    out_cols = heads_here * 3 * HDIM
    local = qkv_weight.reshape(qkv_weight.shape[0], out_cols)
    rows = local.shape[0]
    half_rows = rows // 2
    quarter_rows = half_rows // 2
    core = lax.axis_index("dp") % 2
    mine = lax.dynamic_slice_in_dim(local, core * half_rows, half_rows, 0)
    n_dp = lax.axis_size("dp")

    def send(cells, step):
        return lax.ppermute(cells, "ctx", [(i, step(i)) for i in range(n_ctx)])

    def swap(cells):
        return lax.ppermute(cells, "dp", [(i, i ^ 1) for i in range(n_dp)])

    up = lambda i: (i + 2) % n_ctx
    down = lambda i: (i + n_ctx - 2) % n_ctx
    across = lambda i: i ^ 1
    from_up = (c_idx + n_ctx - 2) % n_ctx
    from_down = (c_idx + 2) % n_ctx
    opposite = (c_idx + 4) % n_ctx
    a_up = send(mine, up)
    a_down = send(mine, down)
    a_across = send(mine, across)
    b_up = send(a_up[:quarter_rows], up)
    b_down = send(a_down[quarter_rows:], down)
    b_across_up = send(a_across, up)
    b_across_down = send(a_across, down)
    c_first = send(b_up, across)
    c_second = send(b_down, across)
    stages = [
        [(a_up, from_up, 0), (a_down, from_down, 0), (a_across, c_idx ^ 1, 0)],
        [(b_up, opposite, 0), (b_down, opposite, quarter_rows),
         (b_across_up, from_up ^ 1, 0), (b_across_down, from_down ^ 1, 0)],
        [(c_first, opposite ^ 1, 0), (c_second, opposite ^ 1, quarter_rows)],
    ]
    stages = [
        (stage, ours, swap(ours))
        for stage, ours in ((s, jnp.concatenate([cells for cells, _, _ in s], 0)) for s in stages)
    ]
    frames = jnp.concatenate([cache, video], 0).reshape(frame_count + 2, tile_rows, tile_cols, cin)
    padded = with_halo(frames, (("head", 1), ("ctx", 2)), 1)
    total = jnp.zeros((frame_count, tile_rows, tile_cols, cmid), jnp.float32)
    for time_tap in range(3):
        for row_tap in range(3):
            slab = padded[time_tap : time_tap + frame_count, row_tap : row_tap + tile_rows]
            stacked = jnp.concatenate(
                [slab[:, :, col_tap : col_tap + tile_cols] for col_tap in range(3)], -1
            )
            total = total + jnp.einsum(
                "fyxc,cd->fyxd",
                stacked,
                conv_weight[time_tap, row_tap],
                preferred_element_type=jnp.float32,
            )
    hidden = silu_act(total + conv_bias).astype(jnp.bfloat16)
    stacked = (
        hidden.reshape(frame_count, tile_rows // 2, 2, tile_cols // 2, 2, cmid)
        .transpose(0, 1, 3, 2, 4, 5)
        .reshape(-1, 4 * cmid)
    )
    reduced = silu_act(jnp.dot(stacked, down_weight, preferred_element_type=jnp.float32)).astype(
        jnp.bfloat16
    )
    reduced = reduced.reshape(frame_count, tile_rows // 2, tile_cols // 2, cmid)
    patches = reduced.reshape(frame_count, tile_rows // 4, 2, tile_cols // 4, 2, cmid).transpose(
        0, 1, 3, 2, 4, 5
    )
    patches = patches.reshape(-1, 4 * cmid)
    half = FREQ // 2
    freqs = jnp.exp(-jnp.log(10000.0) * jnp.arange(half, dtype=jnp.float32) / half)
    angles = step_index[0].astype(jnp.float32) * freqs
    timing = jnp.concatenate([jnp.cos(angles), jnp.sin(angles)]).astype(jnp.bfloat16)
    mod_share = jnp.dot(timing[None, :], mod_weight, preferred_element_type=jnp.float32)[0]
    n_head = lax.axis_size("head")
    n_ctx = lax.axis_size("ctx")
    h_idx = lax.axis_index("head")
    c_idx = lax.axis_index("ctx")
    quarter = D // n_head
    share_width = patch_weight.shape[1]
    share_parts = split3(mod_share).reshape(-1, share_width)
    carried = lax.all_gather(
        jnp.concatenate([patch_weight, share_parts], 0), "ctx", axis=1, tiled=True
    )
    weight_quarter = carried[: patch_weight.shape[0]]
    row_share = (
        carried[patch_weight.shape[0] :]
        .reshape(-1, n_ctx, share_width)
        .transpose(1, 0, 2)
        .reshape(n_ctx, 3, -1)
        .transpose(1, 0, 2)
        .reshape(3, -1)
    )
    row_parts = join3(row_share)
    block_patches = gather_rows(patches, "head").reshape(-1, patches.shape[1])
    embedded = jnp.dot(block_patches, weight_quarter, preferred_element_type=jnp.float32)
    token_count = embedded.shape[0]
    riding = gather_rows(jnp.concatenate([jnp.sum(embedded * embedded, -1), row_parts]), "head")
    squares = riding[:, :token_count]
    modulation = riding[:, token_count:].reshape(-1)
    scale = lax.dynamic_slice_in_dim(modulation, h_idx * quarter, quarter)
    shift = lax.dynamic_slice_in_dim(modulation, D + h_idx * quarter, quarter)
    inverse = lax.rsqrt(jnp.sum(squares, 0) / D + 1e-06)[:, None]
    normed_quarter = (embedded * inverse * (1.0 + scale) + shift).astype(jnp.bfloat16)
    normed = lax.all_gather(normed_quarter, "head", axis=1, tiled=True)
    group_rows = normed.shape[0]
    heads_here = qkv_weight.shape[1]
    out_cols = heads_here * 3 * HDIM
    qkv = None
    for number, (stage, ours, theirs) in enumerate(stages):
        weights = [local] if number == 0 else []
        columns = [lax.dynamic_slice_in_dim(normed, c_idx * rows, rows, 1)] if number == 0 else []
        weights += [ours, theirs]
        for side in (core, 1 - core):
            for cells, block, offset in stage:
                columns.append(
                    lax.dynamic_slice_in_dim(
                        normed, block * rows + side * half_rows + offset, cells.shape[0], 1
                    )
                )
        part = jnp.dot(
            jnp.concatenate(columns, 1),
            jnp.concatenate(weights, 0),
            preferred_element_type=jnp.float32,
        )
        qkv = part if qkv is None else qkv + part
    qkv = qkv.astype(jnp.bfloat16).reshape(group_rows, heads_here, 3, HDIM)
    active = min(heads_here, n_ctx)
    spare = n_ctx - active
    by_part = qkv.transpose(1, 2, 0, 3)
    outgoing = jnp.concatenate([by_part, jnp.zeros((spare,) + by_part.shape[1:], qkv.dtype)], 0)
    triple = lax.all_to_all(outgoing, "ctx", 0, 0, tiled=True)
    keys = triple[:, 1].reshape(-1, HDIM)
    values = triple[:, 2].reshape(-1, HDIM)
    inv_root = 1.0 / jnp.sqrt(jnp.float32(HDIM))

    def one_block(query):
        scores = jnp.dot(query, keys.T, preferred_element_type=jnp.float32) * inv_root
        best = jnp.max(scores, -1)
        probs = jnp.exp(scores - best[:, None])
        denom = jnp.sum(probs, -1)
        accum = jnp.dot(probs.astype(jnp.bfloat16), values, preferred_element_type=jnp.float32)
        return (accum / denom[:, None]).astype(jnp.bfloat16)

    attended = lax.map(one_block, triple[:, 0])
    by_head = lax.all_to_all(attended, "ctx", 0, 0, tiled=True)[:heads_here]
    return by_head.transpose(1, 0, 2).reshape(group_rows, heads_here * HDIM)


def solution(mesh):
    return jax.shard_map(
        shards,
        mesh=mesh,
        in_specs=(
            P("dp", "head", "ctx"),
            P("dp", "head", "ctx"),
            P(),
            P(),
            P(),
            P(None, ("head", "ctx")),
            P("dp"),
            P(None, ("head", "ctx")),
            P("ctx", "head", None, None),
        ),
        out_specs=P(("dp", "ctx"), "head"),
        check_vma=False,
    )
```
